32 devices in a mesh: narrow: 8 (over z, x), wide: 4 (over y, core).
Axes of the slice: x: 2, y: 2, z: 4, core: 2. Of those that a mesh axis runs over, the one named last changes fastest.
Arguments:
- amps: bfloat16 [16, 512, 512], P(None, 'narrow', 'wide'), may hold values from -1 to 1
- left_fit: bfloat16 [64, 512, 256], P(None, 'narrow'), may hold values from -0.375 to 0.375
- right_fit: bfloat16 [512, 512, 256], P('narrow', 'wide'), may hold values from -0.375 to 0.375
- pair_list: int32 [16, 2], P('narrow'), may hold values from 0 to 127, as said below
- occ_energy: float32 [128], replicated, may hold values from -2 to -0.5
- vir_energy: float32 [512], replicated, may hold values from 0.5 to 3
Outputs:
- update: float32 [16, 64, 512], P('narrow', None, 'wide')
The draws below stay inside these ranges and needn't reach their ends.
Inputs may be any that keep to these rules, and one draw needn't show every extreme that they name: `pair_list`: each row (i, j) has i <= j.
All inputs are finite; a program needn't handle non-finite values.
Results may differ from the reference program's by a relative error of at most 0.0029.
Values may be sent and summed in bfloat16 or wider, within the bound.
No kernel may reach another device: no remote copies, remote signals or barrier semaphores. Data moves between devices by JAX's collectives and lax.ppermute only.
A program may use at most 128 MiB of HBM per device.

```python
import jax
import jax.numpy as jnp
from jax import lax

V = 512
NAUX = 256
NOCC = 128
A = 64
P_SIZE = 16


def draw_pair_list(key, part):
    key_one, key_two = jax.random.split(jax.random.fold_in(key, 11))
    first_ids = jax.random.randint(key_one, (P_SIZE,), 0, NOCC)
    second_ids = jax.random.randint(key_two, (P_SIZE,), 0, NOCC)
    lower = jnp.minimum(first_ids, second_ids).at[0].set(0)
    upper = jnp.maximum(first_ids, second_ids).at[0].set(NOCC - 1)
    return jnp.stack([lower, upper], axis=1).astype(jnp.int32)


def strengthened(array, key, source, target, blocks, factor):
    def block_of(dim):
        return (jnp.arange(array.shape[dim]) // (array.shape[dim] // blocks)).reshape((-1,) + (1,) * (array.ndim - 1 - dim))

    near = jax.random.permutation(key, blocks)[block_of(target)]
    second = (block_of(target) + blocks // 2) % blocks
    return jnp.where((block_of(source) == near) | (block_of(source) == second), factor * array, array)


def steps_of(key, extent, pieces, least, largest):
    def one(axis_at, parts):
        steps = jax.random.uniform(jax.random.fold_in(jax.random.fold_in(key, 6), axis_at), (parts,), jnp.float32, least / len(pieces), largest / len(pieces))
        return jnp.repeat(jnp.exp(steps), extent[axis_at] // parts).reshape((-1,) + (1,) * (len(extent) - axis_at - 1))

    loudness = one(*pieces[0])
    for cut in pieces[1:]:
        loudness = loudness * one(*cut)
    return loudness


def gaussian(own_key, shape, scale, reach, cuts=(), held_as=jnp.bfloat16):
    loudness = steps_of(own_key, shape, cuts, -0.22, 0.18) if cuts else 1.0
    values = jax.random.normal(own_key, shape, jnp.float32) * scale * loudness
    return jnp.minimum(jnp.maximum(values, -reach), reach).astype(held_as)


def heavy_noise(rng, shape, spread, reach, shards, heavy, kind=jnp.bfloat16):
    entries = spread * jax.random.normal(rng, shape, jnp.float32)
    if shards:
        entries = entries * steps_of(rng, shape, shards, -0.22, 0.18)
    return jnp.clip(strengthened(entries, jax.random.fold_in(rng, 3), *heavy), -reach, reach).astype(kind)


def setup_inputs(seed: int = 0) -> dict:
    streams_of = jax.random.split(jax.random.key(seed), 7)
    return {
        "amps": gaussian(streams_of[0], (P_SIZE, V, V), (V // 16) ** -0.5, 1.0, ((1, 8), (2, 4))),
        "left_fit": gaussian(streams_of[1], (A, V, NAUX), NAUX ** -0.5, 0.375, ((1, 8),)),
        "right_fit": heavy_noise(streams_of[2], (V, V, NAUX), V ** -0.5, 0.375, ((0, 8), (1, 4)), (1, 0, 8, 2.0)),
        "pair_list": draw_pair_list(jax.random.fold_in(streams_of[6], 71), 0),
        "occ_energy": jnp.clip(jax.random.uniform(streams_of[4], (NOCC,), jnp.float32, -2.0, -0.5), -2.0, -0.5),
        "vir_energy": jnp.clip(jax.random.uniform(streams_of[5], (V,), jnp.float32, 0.5, 3.0), 0.5, 3.0),
    }


def reference(amps, left_fit, right_fit, pair_list, occ_energy, vir_energy):
    left_wide = left_fit.astype(jnp.float32)
    right_wide = right_fit.astype(jnp.float32)

    def one_pair(amp_row):
        inter = jnp.einsum("acq,cd->adq", left_wide, amp_row.astype(jnp.float32))
        inter = lax.optimization_barrier(inter.astype(jnp.bfloat16)).astype(jnp.float32)
        return jnp.einsum("adq,bdq->ab", inter, right_wide)

    ladder = lax.map(one_pair, amps)
    pair_energy = occ_energy[pair_list[:, 0]] + occ_energy[pair_list[:, 1]]
    denominator = pair_energy[:, None, None] - vir_energy[:A][None, :, None] - vir_energy[None, None, :]
    return ladder / denominator
```

```python
import jax
import jax.numpy as jnp
from jax import lax
from jax.sharding import PartitionSpec as P

GROUPS = 2


def make_body(n_narrow, n_wide):
    span = n_narrow // GROUPS

    def body(amps, left_fit, right_fit, pair_list, occ_energy, vir_energy):
        n = lax.axis_index("narrow")
        w = lax.axis_index("wide")
        r = n % span
        g = n // span
        b_blk, d_blk, aux = right_fit.shape
        q_blk = aux // span
        rows, c_blk, _ = left_fit.shape
        pairs = amps.shape[0]
        vir_total = b_blk * n_narrow

        amps_all = lax.all_gather(amps, "narrow", axis=1, tiled=True)

        c_sub = c_blk // n_wide
        left_part = lax.dynamic_slice_in_dim(left_fit, w * c_sub, c_sub, 1)
        left_part = left_part.reshape(rows, c_sub, span, q_blk).transpose(2, 0, 1, 3)
        left_send = jnp.concatenate([left_part] * GROUPS, axis=0)
        left_recv = lax.all_to_all(left_send, "narrow", 0, 0, tiled=True)
        left_all = lax.all_gather(left_recv, "wide", axis=0, tiled=False)
        left_all = left_all.transpose(2, 1, 0, 3, 4).reshape(rows, c_blk * n_narrow, q_blk)

        right_split = right_fit.reshape(b_blk, d_blk, span, q_blk)
        chunks = []
        for shift in range(span):
            dest = (r + shift) % span
            piece = lax.dynamic_index_in_dim(right_split, dest, 2, keepdims=False)
            if shift:
                perm = [
                    (gg * span + i, gg * span + (i + shift) % span)
                    for gg in range(GROUPS)
                    for i in range(span)
                ]
                piece = lax.ppermute(piece, "narrow", perm)
            chunks.append(piece)

        inter = jnp.einsum(
            "acq,pcd->padq", left_all, amps_all, preferred_element_type=jnp.float32
        ).astype(jnp.bfloat16)

        ladder = jnp.zeros((pairs, rows, vir_total), jnp.float32)
        for shift, piece in enumerate(chunks):
            part = jnp.einsum(
                "padq,bdq->pab", inter, piece, preferred_element_type=jnp.float32
            )
            src = g * span + (r - shift) % span
            ladder = lax.dynamic_update_slice_in_dim(ladder, part, src * b_blk, 2)

        ladder = lax.psum_scatter(ladder, "wide", scatter_dimension=2, tiled=True)
        ladder = lax.psum_scatter(ladder, "narrow", scatter_dimension=0, tiled=True)

        local_cols = ladder.shape[2]
        occ_ids = jnp.arange(occ_energy.shape[0], dtype=jnp.int32)
        occ_first = jnp.sum(
            jnp.where(pair_list[:, 0:1] == occ_ids[None, :], occ_energy[None, :], 0.0), axis=1
        )
        occ_second = jnp.sum(
            jnp.where(pair_list[:, 1:2] == occ_ids[None, :], occ_energy[None, :], 0.0), axis=1
        )
        vir_cols = lax.dynamic_slice_in_dim(vir_energy, w * local_cols, local_cols, 0)
        vir_rows = vir_energy[:rows]
        denominator = (
            (occ_first + occ_second)[:, None, None] - vir_rows[None, :, None] - vir_cols[None, None, :]
        )
        return ladder / denominator

    return body


def solution(mesh):
    return jax.shard_map(
        make_body(mesh.shape["narrow"], mesh.shape["wide"]),
        mesh=mesh,
        in_specs=(
            P(None, "narrow", "wide"),
            P(None, "narrow", None),
            P("narrow", "wide", None),
            P("narrow", None),
            P(),
            P(),
        ),
        out_specs=P("narrow", None, "wide"),
        check_vma=False,
    )
```

```python
import jax
import jax.numpy as jnp
from jax import lax
from jax.sharding import PartitionSpec as P

GROUPS = 2


def make_body(n_narrow, n_wide):
    span = n_narrow // GROUPS

    def body(amps, left_fit, right_fit, pair_list, occ_energy, vir_energy):
        n = lax.axis_index("narrow")
        w = lax.axis_index("wide")
        r = n % span
        g = n // span
        b_blk, d_blk, aux = right_fit.shape
        q_blk = aux // span
        rows, c_blk, _ = left_fit.shape
        pairs = amps.shape[0]
        vir_total = b_blk * n_narrow

        amps_all = lax.all_gather(amps, "narrow", axis=1, tiled=True)

        c_sub = c_blk // n_wide
        left_part = lax.dynamic_slice_in_dim(left_fit, w * c_sub, c_sub, 1)
        left_part = left_part.reshape(rows, c_sub, span, q_blk).transpose(2, 0, 1, 3)
        left_send = jnp.concatenate([left_part] * GROUPS, axis=0)
        left_recv = lax.all_to_all(left_send, "narrow", 0, 0, tiled=True)
        left_all = lax.all_gather(left_recv, "wide", axis=0, tiled=False)
        left_all = left_all.transpose(2, 1, 0, 3, 4).reshape(rows, c_blk * n_narrow, q_blk)

        right_split = right_fit.reshape(b_blk, d_blk, span, q_blk)
        chunks = []
        for shift in range(span):
            dest = (r + shift) % span
            piece = lax.dynamic_index_in_dim(right_split, dest, 2, keepdims=False)
            if shift:
                perm = [
                    (gg * span + i, gg * span + (i + shift) % span)
                    for gg in range(GROUPS)
                    for i in range(span)
                ]
                piece = lax.ppermute(piece, "narrow", perm)
            chunks.append(piece)

        inter = jnp.einsum(
            "acq,pcd->padq", left_all, amps_all, preferred_element_type=jnp.float32
        ).astype(jnp.bfloat16)

        right_group = jnp.concatenate(chunks, axis=0)
        part = lax.dot_general(
            inter.reshape(pairs * rows, d_blk * q_blk),
            right_group.reshape(span * b_blk, d_blk * q_blk),
            (((1,), (1,)), ((), ())),
            preferred_element_type=jnp.float32,
        ).reshape(pairs, rows, span, b_blk)
        flipped = jnp.concatenate(
            [part[:, :, (span - k) % span : (span - k) % span + 1] for k in range(span)] * 2, axis=2
        )
        ordered = lax.dynamic_slice_in_dim(flipped, span - r, span, 2)
        ordered = ordered.reshape(pairs, rows, span * b_blk)
        pad = jnp.zeros((pairs, rows, (GROUPS - 1) * span * b_blk), jnp.float32)
        padded = jnp.concatenate([pad, ordered, pad], axis=2)
        ladder = lax.dynamic_slice_in_dim(
            padded, (GROUPS - 1 - g) * span * b_blk, vir_total, 2
        )

        ladder = lax.psum_scatter(ladder, "wide", scatter_dimension=2, tiled=True)
        ladder = lax.psum_scatter(ladder, "narrow", scatter_dimension=0, tiled=True)

        local_cols = ladder.shape[2]
        occ_ids = jnp.arange(occ_energy.shape[0], dtype=jnp.int32)
        occ_first = jnp.sum(
            jnp.where(pair_list[:, 0:1] == occ_ids[None, :], occ_energy[None, :], 0.0), axis=1
        )
        occ_second = jnp.sum(
            jnp.where(pair_list[:, 1:2] == occ_ids[None, :], occ_energy[None, :], 0.0), axis=1
        )
        vir_cols = lax.dynamic_slice_in_dim(vir_energy, w * local_cols, local_cols, 0)
        vir_rows = vir_energy[:rows]
        denominator = (
            (occ_first + occ_second)[:, None, None] - vir_rows[None, :, None] - vir_cols[None, None, :]
        )
        return ladder / denominator

    return body


def solution(mesh):
    return jax.shard_map(
        make_body(mesh.shape["narrow"], mesh.shape["wide"]),
        mesh=mesh,
        in_specs=(
            P(None, "narrow", "wide"),
            P(None, "narrow", None),
            P("narrow", "wide", None),
            P("narrow", None),
            P(),
            P(),
        ),
        out_specs=P("narrow", None, "wide"),
        check_vma=False,
    )
```

```python
import jax
import jax.numpy as jnp
from jax import lax
from jax.sharding import PartitionSpec as P

GROUPS = 2


def make_body(n_narrow, n_wide):
    span = n_narrow // GROUPS

    def body(amps, left_fit, right_fit, pair_list, occ_energy, vir_energy):
        n = lax.axis_index("narrow")
        w = lax.axis_index("wide")
        r = n % span
        g = n // span
        b_blk, d_blk, aux = right_fit.shape
        q_blk = aux // span
        rows, c_blk, _ = left_fit.shape
        pairs = amps.shape[0]
        vir_total = b_blk * n_narrow

        amps_all = lax.all_gather(amps, "narrow", axis=1, tiled=True)

        c_sub = c_blk // n_wide
        left_part = lax.dynamic_slice_in_dim(left_fit, w * c_sub, c_sub, 1)
        left_part = left_part.reshape(rows, c_sub, span, q_blk).transpose(2, 0, 1, 3)
        left_send = jnp.concatenate([left_part] * GROUPS, axis=0)
        left_recv = lax.all_to_all(left_send, "narrow", 0, 0, tiled=True)
        left_all = lax.all_gather(left_recv, "wide", axis=0, tiled=False)
        left_all = left_all.transpose(2, 1, 0, 3, 4).reshape(rows, c_blk * n_narrow, q_blk)

        right_split = right_fit.reshape(b_blk, d_blk, span, q_blk)
        chunks = []
        for shift in range(span):
            dest = (r + shift) % span
            piece = lax.dynamic_index_in_dim(right_split, dest, 2, keepdims=False)
            if shift:
                perm = [
                    (gg * span + i, gg * span + (i + shift) % span)
                    for gg in range(GROUPS)
                    for i in range(span)
                ]
                piece = lax.ppermute(piece, "narrow", perm)
            chunks.append(piece)

        inter = jnp.einsum(
            "acq,pcd->padq", left_all, amps_all, preferred_element_type=jnp.float32
        ).astype(jnp.bfloat16)

        right_group = jnp.concatenate(chunks, axis=0)
        part = jnp.einsum(
            "padq,bdq->pab", inter, right_group, preferred_element_type=jnp.float32
        ).reshape(pairs, rows, span, b_blk)
        flipped = jnp.concatenate(
            [part[:, :, (span - k) % span : (span - k) % span + 1] for k in range(span)] * 2, axis=2
        )
        ordered = lax.dynamic_slice_in_dim(flipped, span - r, span, 2)
        ordered = ordered.reshape(pairs, rows, span * b_blk)
        pad = jnp.zeros((pairs, rows, (GROUPS - 1) * span * b_blk), jnp.float32)
        padded = jnp.concatenate([pad, ordered, pad], axis=2)
        ladder = lax.dynamic_slice_in_dim(
            padded, (GROUPS - 1 - g) * span * b_blk, vir_total, 2
        )

        ladder = lax.psum_scatter(ladder, "wide", scatter_dimension=2, tiled=True)
        ladder = lax.psum_scatter(ladder, "narrow", scatter_dimension=0, tiled=True)

        local_cols = ladder.shape[2]
        occ_ids = jnp.arange(occ_energy.shape[0], dtype=jnp.int32)
        occ_first = jnp.sum(
            jnp.where(pair_list[:, 0:1] == occ_ids[None, :], occ_energy[None, :], 0.0), axis=1
        )
        occ_second = jnp.sum(
            jnp.where(pair_list[:, 1:2] == occ_ids[None, :], occ_energy[None, :], 0.0), axis=1
        )
        vir_cols = lax.dynamic_slice_in_dim(vir_energy, w * local_cols, local_cols, 0)
        vir_rows = vir_energy[:rows]
        denominator = (
            (occ_first + occ_second)[:, None, None] - vir_rows[None, :, None] - vir_cols[None, None, :]
        )
        return ladder / denominator

    return body


def solution(mesh):
    return jax.shard_map(
        make_body(mesh.shape["narrow"], mesh.shape["wide"]),
        mesh=mesh,
        in_specs=(
            P(None, "narrow", "wide"),
            P(None, "narrow", None),
            P("narrow", "wide", None),
            P("narrow", None),
            P(),
            P(),
        ),
        out_specs=P("narrow", None, "wide"),
        check_vma=False,
    )
```

```python
import jax
import jax.numpy as jnp
from jax import lax
from jax.sharding import PartitionSpec as P

GROUPS = 2


def make_body(n_narrow, n_wide):
    span = n_narrow // GROUPS

    def body(amps, left_fit, right_fit, pair_list, occ_energy, vir_energy):
        n = lax.axis_index("narrow")
        w = lax.axis_index("wide")
        r = n % span
        g = n // span
        b_blk, d_blk, aux = right_fit.shape
        q_blk = aux // span
        rows, c_blk, _ = left_fit.shape
        pairs = amps.shape[0]
        vir_total = b_blk * n_narrow

        amps_all = lax.all_gather(amps, "narrow", axis=1, tiled=True)

        c_sub = c_blk // n_wide
        left_part = lax.dynamic_slice_in_dim(left_fit, w * c_sub, c_sub, 1)
        left_part = left_part.reshape(rows, c_sub, span, q_blk).transpose(2, 0, 1, 3)
        left_send = jnp.concatenate([left_part] * GROUPS, axis=0)
        left_recv = lax.all_to_all(left_send, "narrow", 0, 0, tiled=True)
        left_all = lax.all_gather(left_recv, "wide", axis=0, tiled=False)
        left_all = left_all.transpose(2, 1, 0, 3, 4).reshape(rows, c_blk * n_narrow, q_blk)

        right_split = right_fit.reshape(b_blk, d_blk, span, q_blk)
        chunks = []
        for shift in range(span):
            dest = (r + shift) % span
            piece = lax.dynamic_index_in_dim(right_split, dest, 2, keepdims=False)
            if shift:
                perm = [
                    (gg * span + i, gg * span + (i + shift) % span)
                    for gg in range(GROUPS)
                    for i in range(span)
                ]
                piece = lax.ppermute(piece, "narrow", perm)
            chunks.append(piece)

        inter = jnp.einsum(
            "acq,pcd->padq", left_all, amps_all, preferred_element_type=jnp.float32
        ).astype(jnp.bfloat16)

        right_group = jnp.concatenate(chunks, axis=0)
        part = jnp.einsum(
            "padq,bdq->pab", inter, right_group, preferred_element_type=jnp.float32
        )
        part = lax.psum_scatter(part, "wide", scatter_dimension=0, tiled=True)
        pairs_w = part.shape[0]
        part = part.reshape(pairs_w, rows, span, b_blk)
        flipped = jnp.concatenate(
            [part[:, :, (span - k) % span : (span - k) % span + 1] for k in range(span)] * 2, axis=2
        )
        ordered = lax.dynamic_slice_in_dim(flipped, span - r, span, 2)
        n_per_w = n_narrow // n_wide
        w_per_g = n_wide // GROUPS
        cols = span * b_blk // w_per_g
        ordered = ordered.reshape(n_per_w, pairs_w // n_per_w, rows, w_per_g, cols)
        ladder = None
        for t in range(span):
            k = (t + r) % span
            piece = lax.dynamic_index_in_dim(ordered, k // w_per_g, 0, keepdims=False)
            piece = lax.dynamic_index_in_dim(piece, k % w_per_g, 2, keepdims=False)
            perm = []
            for gg in range(GROUPS):
                for rr in range(span):
                    for ww in range(n_wide):
                        kk = (t + rr) % span
                        dst_n = ww * n_per_w + kk // w_per_g
                        dst_w = gg * w_per_g + kk % w_per_g
                        perm.append(((gg * span + rr) * n_wide + ww, dst_n * n_wide + dst_w))
            piece = lax.ppermute(piece, ("narrow", "wide"), perm)
            ladder = piece if ladder is None else ladder + piece

        local_cols = ladder.shape[2]
        occ_ids = jnp.arange(occ_energy.shape[0], dtype=jnp.int32)
        occ_first = jnp.sum(
            jnp.where(pair_list[:, 0:1] == occ_ids[None, :], occ_energy[None, :], 0.0), axis=1
        )
        occ_second = jnp.sum(
            jnp.where(pair_list[:, 1:2] == occ_ids[None, :], occ_energy[None, :], 0.0), axis=1
        )
        vir_cols = lax.dynamic_slice_in_dim(vir_energy, w * local_cols, local_cols, 0)
        vir_rows = vir_energy[:rows]
        denominator = (
            (occ_first + occ_second)[:, None, None] - vir_rows[None, :, None] - vir_cols[None, None, :]
        )
        return ladder / denominator

    return body


def solution(mesh):
    return jax.shard_map(
        make_body(mesh.shape["narrow"], mesh.shape["wide"]),
        mesh=mesh,
        in_specs=(
            P(None, "narrow", "wide"),
            P(None, "narrow", None),
            P("narrow", "wide", None),
            P("narrow", None),
            P(),
            P(),
        ),
        out_specs=P("narrow", None, "wide"),
        check_vma=False,
    )
```

```python
import jax
import jax.numpy as jnp
from jax import lax
from jax.sharding import PartitionSpec as P

GROUPS = 2


def make_body(n_narrow, n_wide):
    span = n_narrow // GROUPS

    def body(amps, left_fit, right_fit, pair_list, occ_energy, vir_energy):
        n = lax.axis_index("narrow")
        w = lax.axis_index("wide")
        r = n % span
        g = n // span
        b_blk, d_blk, aux = right_fit.shape
        q_blk = aux // span
        rows, c_blk, _ = left_fit.shape
        pairs = amps.shape[0]
        vir_total = b_blk * n_narrow

        def shifted(x, shift):
            if not shift:
                return x
            perm = [(i, (i + shift) % n_narrow) for i in range(n_narrow)]
            return lax.ppermute(x, "narrow", perm)

        amps_all = jnp.stack([shifted(amps, s) for s in range(n_narrow)], axis=1)
        amps_all = amps_all.reshape(pairs, n_narrow * c_blk, amps.shape[2])

        c_sub = c_blk // n_wide
        left_part = lax.dynamic_slice_in_dim(left_fit, w * c_sub, c_sub, 1)
        left_part = left_part.reshape(rows, c_sub, span, q_blk).transpose(2, 0, 1, 3)
        left_recv = []
        for shift in range(n_narrow):
            dest = ((n + shift) % n_narrow) % span
            left_recv.append(shifted(lax.dynamic_index_in_dim(left_part, dest, 0, keepdims=False), shift))
        left_recv = jnp.stack(left_recv, axis=0)
        left_all = lax.all_gather(left_recv, "wide", axis=0, tiled=False)
        left_all = left_all.transpose(2, 1, 0, 3, 4).reshape(rows, c_blk * n_narrow, q_blk)

        right_split = right_fit.reshape(b_blk, d_blk, span, q_blk)
        chunks = []
        for shift in range(span):
            dest = (r + shift) % span
            piece = lax.dynamic_index_in_dim(right_split, dest, 2, keepdims=False)
            if shift:
                perm = [
                    (gg * span + i, gg * span + (i + shift) % span)
                    for gg in range(GROUPS)
                    for i in range(span)
                ]
                piece = lax.ppermute(piece, "narrow", perm)
            chunks.append(piece)

        inter = jnp.einsum(
            "acq,pcd->padq", left_all, amps_all, preferred_element_type=jnp.float32
        ).astype(jnp.bfloat16)

        right_group = jnp.concatenate(chunks, axis=0)
        part = jnp.einsum(
            "padq,bdq->pab", inter, right_group, preferred_element_type=jnp.float32
        )
        part = lax.psum_scatter(part, "wide", scatter_dimension=0, tiled=True)
        pairs_w = part.shape[0]
        part = part.reshape(pairs_w, rows, span, b_blk)
        flipped = jnp.concatenate(
            [part[:, :, (span - k) % span : (span - k) % span + 1] for k in range(span)] * 2, axis=2
        )
        ordered = lax.dynamic_slice_in_dim(flipped, span - r, span, 2)
        n_per_w = n_narrow // n_wide
        w_per_g = n_wide // GROUPS
        cols = span * b_blk // w_per_g
        ordered = ordered.reshape(n_per_w, pairs_w // n_per_w, rows, w_per_g, cols)
        ladder = None
        for t in range(span):
            k = (t + r) % span
            piece = lax.dynamic_index_in_dim(ordered, k // w_per_g, 0, keepdims=False)
            piece = lax.dynamic_index_in_dim(piece, k % w_per_g, 2, keepdims=False)
            perm = []
            for gg in range(GROUPS):
                for rr in range(span):
                    for ww in range(n_wide):
                        kk = (t + rr) % span
                        dst_n = ww * n_per_w + kk // w_per_g
                        dst_w = gg * w_per_g + kk % w_per_g
                        perm.append(((gg * span + rr) * n_wide + ww, dst_n * n_wide + dst_w))
            piece = lax.ppermute(piece, ("narrow", "wide"), perm)
            ladder = piece if ladder is None else ladder + piece

        local_cols = ladder.shape[2]
        occ_ids = jnp.arange(occ_energy.shape[0], dtype=jnp.int32)
        occ_first = jnp.sum(
            jnp.where(pair_list[:, 0:1] == occ_ids[None, :], occ_energy[None, :], 0.0), axis=1
        )
        occ_second = jnp.sum(
            jnp.where(pair_list[:, 1:2] == occ_ids[None, :], occ_energy[None, :], 0.0), axis=1
        )
        vir_cols = lax.dynamic_slice_in_dim(vir_energy, w * local_cols, local_cols, 0)
        vir_rows = vir_energy[:rows]
        denominator = (
            (occ_first + occ_second)[:, None, None] - vir_rows[None, :, None] - vir_cols[None, None, :]
        )
        return ladder / denominator

    return body


def solution(mesh):
    return jax.shard_map(
        make_body(mesh.shape["narrow"], mesh.shape["wide"]),
        mesh=mesh,
        in_specs=(
            P(None, "narrow", "wide"),
            P(None, "narrow", None),
            P("narrow", "wide", None),
            P("narrow", None),
            P(),
            P(),
        ),
        out_specs=P("narrow", None, "wide"),
        check_vma=False,
    )
```

```python
import jax
import jax.numpy as jnp
from jax import lax
from jax.sharding import PartitionSpec as P

GROUPS = 2


def make_body(n_narrow, n_wide):
    span = n_narrow // GROUPS

    def body(amps, left_fit, right_fit, pair_list, occ_energy, vir_energy):
        n = lax.axis_index("narrow")
        w = lax.axis_index("wide")
        r = n % span
        g = n // span
        b_blk, d_blk, aux = right_fit.shape
        q_blk = aux // span
        rows, c_blk, _ = left_fit.shape
        pairs = amps.shape[0]
        vir_total = b_blk * n_narrow

        amps_blocks = [amps]
        for shift in range(1, n_narrow):
            perm = [(i, (i + shift) % n_narrow) for i in range(n_narrow)]
            amps_blocks.append(lax.ppermute(amps, "narrow", perm))
        amps_all = jnp.stack(amps_blocks, axis=1)

        c_sub = c_blk // n_wide
        left_part = lax.dynamic_slice_in_dim(left_fit, w * c_sub, c_sub, 1)
        left_part = left_part.reshape(rows, c_sub, span, q_blk).transpose(2, 0, 1, 3)
        left_send = jnp.concatenate([left_part] * GROUPS, axis=0)
        left_recv = lax.all_to_all(left_send, "narrow", 0, 0, tiled=True)
        left_all = lax.all_gather(left_recv, "wide", axis=0, tiled=False)
        left_all = left_all.transpose(2, 1, 0, 3, 4).reshape(rows, c_blk * n_narrow, q_blk)

        right_split = right_fit.reshape(b_blk, d_blk, span, q_blk)
        chunks = []
        for shift in range(span):
            dest = (r + shift) % span
            piece = lax.dynamic_index_in_dim(right_split, dest, 2, keepdims=False)
            if shift:
                perm = [
                    (gg * span + i, gg * span + (i + shift) % span)
                    for gg in range(GROUPS)
                    for i in range(span)
                ]
                piece = lax.ppermute(piece, "narrow", perm)
            chunks.append(piece)

        left_blocks = left_all.reshape(rows, n_narrow, c_blk, q_blk)
        left_flip = jnp.concatenate(
            [left_blocks[:, (n_narrow - k) % n_narrow : (n_narrow - k) % n_narrow + 1] for k in range(n_narrow)] * 2,
            axis=1,
        )
        left_shifted = lax.dynamic_slice_in_dim(left_flip, n_narrow - n, n_narrow, 1)
        inter = jnp.einsum(
            "ankq,pnkd->padq", left_shifted, amps_all, preferred_element_type=jnp.float32
        ).astype(jnp.bfloat16)

        right_group = jnp.concatenate(chunks, axis=0)
        part = jnp.einsum(
            "padq,bdq->pab", inter, right_group, preferred_element_type=jnp.float32
        )
        part = lax.psum_scatter(part, "wide", scatter_dimension=0, tiled=True)
        pairs_w = part.shape[0]
        part = part.reshape(pairs_w, rows, span, b_blk)
        flipped = jnp.concatenate(
            [part[:, :, (span - k) % span : (span - k) % span + 1] for k in range(span)] * 2, axis=2
        )
        ordered = lax.dynamic_slice_in_dim(flipped, span - r, span, 2)
        n_per_w = n_narrow // n_wide
        w_per_g = n_wide // GROUPS
        cols = span * b_blk // w_per_g
        ordered = ordered.reshape(n_per_w, pairs_w // n_per_w, rows, w_per_g, cols)
        ladder = None
        for t in range(span):
            k = (t + r) % span
            piece = lax.dynamic_index_in_dim(ordered, k // w_per_g, 0, keepdims=False)
            piece = lax.dynamic_index_in_dim(piece, k % w_per_g, 2, keepdims=False)
            perm = []
            for gg in range(GROUPS):
                for rr in range(span):
                    for ww in range(n_wide):
                        kk = (t + rr) % span
                        dst_n = ww * n_per_w + kk // w_per_g
                        dst_w = gg * w_per_g + kk % w_per_g
                        perm.append(((gg * span + rr) * n_wide + ww, dst_n * n_wide + dst_w))
            piece = lax.ppermute(piece, ("narrow", "wide"), perm)
            ladder = piece if ladder is None else ladder + piece

        local_cols = ladder.shape[2]
        occ_ids = jnp.arange(occ_energy.shape[0], dtype=jnp.int32)
        occ_first = jnp.sum(
            jnp.where(pair_list[:, 0:1] == occ_ids[None, :], occ_energy[None, :], 0.0), axis=1
        )
        occ_second = jnp.sum(
            jnp.where(pair_list[:, 1:2] == occ_ids[None, :], occ_energy[None, :], 0.0), axis=1
        )
        vir_cols = lax.dynamic_slice_in_dim(vir_energy, w * local_cols, local_cols, 0)
        vir_rows = vir_energy[:rows]
        denominator = (
            (occ_first + occ_second)[:, None, None] - vir_rows[None, :, None] - vir_cols[None, None, :]
        )
        return ladder / denominator

    return body


def solution(mesh):
    return jax.shard_map(
        make_body(mesh.shape["narrow"], mesh.shape["wide"]),
        mesh=mesh,
        in_specs=(
            P(None, "narrow", "wide"),
            P(None, "narrow", None),
            P("narrow", "wide", None),
            P("narrow", None),
            P(),
            P(),
        ),
        out_specs=P("narrow", None, "wide"),
        check_vma=False,
    )
```

```python
import jax
import jax.numpy as jnp
from jax import lax
from jax.sharding import PartitionSpec as P

GROUPS = 2


def make_body(n_narrow, n_wide):
    span = n_narrow // GROUPS

    def body(amps, left_fit, right_fit, pair_list, occ_energy, vir_energy):
        n = lax.axis_index("narrow")
        w = lax.axis_index("wide")
        r = n % span
        g = n // span
        b_blk, d_blk, aux = right_fit.shape
        q_blk = aux // span
        rows, c_blk, _ = left_fit.shape
        pairs = amps.shape[0]
        vir_total = b_blk * n_narrow

        amps_blocks = [amps]
        for shift in range(1, n_narrow):
            perm = [(i, (i + shift) % n_narrow) for i in range(n_narrow)]
            amps_blocks.append(lax.ppermute(amps, "narrow", perm))
        amps_rev = [amps_blocks[(n_narrow - j) % n_narrow] for j in range(n_narrow)]
        amps_all = lax.dynamic_slice_in_dim(
            jnp.concatenate(amps_rev * 2, axis=1), (n_narrow - n) * c_blk, n_narrow * c_blk, 1
        )

        c_sub = c_blk // n_wide
        left_part = lax.dynamic_slice_in_dim(left_fit, w * c_sub, c_sub, 1)
        left_part = left_part.reshape(rows, c_sub, span, q_blk).transpose(2, 0, 1, 3)
        left_send = jnp.concatenate([left_part] * GROUPS, axis=0)
        left_recv = lax.all_to_all(left_send, "narrow", 0, 0, tiled=True)
        left_all = lax.all_gather(left_recv, "wide", axis=0, tiled=False)
        left_all = left_all.transpose(2, 1, 0, 3, 4).reshape(rows, c_blk * n_narrow, q_blk)

        right_split = right_fit.reshape(b_blk, d_blk, span, q_blk)
        chunks = []
        for shift in range(span):
            dest = (r + shift) % span
            piece = lax.dynamic_index_in_dim(right_split, dest, 2, keepdims=False)
            if shift:
                perm = [
                    (gg * span + i, gg * span + (i + shift) % span)
                    for gg in range(GROUPS)
                    for i in range(span)
                ]
                piece = lax.ppermute(piece, "narrow", perm)
            chunks.append(piece)

        inter = jnp.einsum(
            "acq,pcd->padq", left_all, amps_all, preferred_element_type=jnp.float32
        ).astype(jnp.bfloat16)

        right_group = jnp.concatenate(chunks, axis=0)
        part = jnp.einsum(
            "padq,bdq->pab", inter, right_group, preferred_element_type=jnp.float32
        )
        part = lax.psum_scatter(part, "wide", scatter_dimension=0, tiled=True)
        pairs_w = part.shape[0]
        part = part.reshape(pairs_w, rows, span, b_blk)
        flipped = jnp.concatenate(
            [part[:, :, (span - k) % span : (span - k) % span + 1] for k in range(span)] * 2, axis=2
        )
        ordered = lax.dynamic_slice_in_dim(flipped, span - r, span, 2)
        n_per_w = n_narrow // n_wide
        w_per_g = n_wide // GROUPS
        cols = span * b_blk // w_per_g
        ordered = ordered.reshape(n_per_w, pairs_w // n_per_w, rows, w_per_g, cols)
        ladder = None
        for t in range(span):
            k = (t + r) % span
            piece = lax.dynamic_index_in_dim(ordered, k // w_per_g, 0, keepdims=False)
            piece = lax.dynamic_index_in_dim(piece, k % w_per_g, 2, keepdims=False)
            perm = []
            for gg in range(GROUPS):
                for rr in range(span):
                    for ww in range(n_wide):
                        kk = (t + rr) % span
                        dst_n = ww * n_per_w + kk // w_per_g
                        dst_w = gg * w_per_g + kk % w_per_g
                        perm.append(((gg * span + rr) * n_wide + ww, dst_n * n_wide + dst_w))
            piece = lax.ppermute(piece, ("narrow", "wide"), perm)
            ladder = piece if ladder is None else ladder + piece

        local_cols = ladder.shape[2]
        occ_ids = jnp.arange(occ_energy.shape[0], dtype=jnp.int32)
        occ_first = jnp.sum(
            jnp.where(pair_list[:, 0:1] == occ_ids[None, :], occ_energy[None, :], 0.0), axis=1
        )
        occ_second = jnp.sum(
            jnp.where(pair_list[:, 1:2] == occ_ids[None, :], occ_energy[None, :], 0.0), axis=1
        )
        vir_cols = lax.dynamic_slice_in_dim(vir_energy, w * local_cols, local_cols, 0)
        vir_rows = vir_energy[:rows]
        denominator = (
            (occ_first + occ_second)[:, None, None] - vir_rows[None, :, None] - vir_cols[None, None, :]
        )
        return ladder / denominator

    return body


def solution(mesh):
    return jax.shard_map(
        make_body(mesh.shape["narrow"], mesh.shape["wide"]),
        mesh=mesh,
        in_specs=(
            P(None, "narrow", "wide"),
            P(None, "narrow", None),
            P("narrow", "wide", None),
            P("narrow", None),
            P(),
            P(),
        ),
        out_specs=P("narrow", None, "wide"),
        check_vma=False,
    )
```

```python
import jax
import jax.numpy as jnp
from jax import lax
from jax.sharding import PartitionSpec as P

GROUPS = 2


def make_body(n_narrow, n_wide):
    span = n_narrow // GROUPS

    def body(amps, left_fit, right_fit, pair_list, occ_energy, vir_energy):
        n = lax.axis_index("narrow")
        w = lax.axis_index("wide")
        r = n % span
        g = n // span
        b_blk, d_blk, aux = right_fit.shape
        q_blk = aux // span
        rows, c_blk, _ = left_fit.shape
        pairs = amps.shape[0]
        vir_total = b_blk * n_narrow

        amps_all = lax.all_gather(amps, "narrow", axis=1, tiled=True)

        c_sub = c_blk // n_wide
        left_part = lax.dynamic_slice_in_dim(left_fit, w * c_sub, c_sub, 1)
        left_part = left_part.reshape(rows, c_sub, span, q_blk).transpose(2, 0, 1, 3)
        left_blocks = []
        for shift in range(n_narrow):
            dest = ((n + shift) % n_narrow) % span
            piece = lax.dynamic_index_in_dim(left_part, dest, 0, keepdims=True)
            if shift:
                perm = [(i, (i + shift) % n_narrow) for i in range(n_narrow)]
                piece = lax.ppermute(piece, "narrow", perm)
            left_blocks.append(piece)
        left_rev = [left_blocks[(n_narrow - j) % n_narrow] for j in range(n_narrow)]
        left_recv = lax.dynamic_slice_in_dim(
            jnp.concatenate(left_rev * 2, axis=0), n_narrow - n, n_narrow, 0
        )
        left_all = lax.all_gather(left_recv, "wide", axis=0, tiled=False)
        left_all = left_all.transpose(2, 1, 0, 3, 4).reshape(rows, c_blk * n_narrow, q_blk)

        right_split = right_fit.reshape(b_blk, d_blk, span, q_blk)
        chunks = []
        for shift in range(span):
            dest = (r + shift) % span
            piece = lax.dynamic_index_in_dim(right_split, dest, 2, keepdims=False)
            if shift:
                perm = [
                    (gg * span + i, gg * span + (i + shift) % span)
                    for gg in range(GROUPS)
                    for i in range(span)
                ]
                piece = lax.ppermute(piece, "narrow", perm)
            chunks.append(piece)

        inter = jnp.einsum(
            "acq,pcd->padq", left_all, amps_all, preferred_element_type=jnp.float32
        ).astype(jnp.bfloat16)

        right_group = jnp.concatenate(chunks, axis=0)
        part = jnp.einsum(
            "padq,bdq->pab", inter, right_group, preferred_element_type=jnp.float32
        )
        part = lax.psum_scatter(part, "wide", scatter_dimension=0, tiled=True)
        pairs_w = part.shape[0]
        part = part.reshape(pairs_w, rows, span, b_blk)
        flipped = jnp.concatenate(
            [part[:, :, (span - k) % span : (span - k) % span + 1] for k in range(span)] * 2, axis=2
        )
        ordered = lax.dynamic_slice_in_dim(flipped, span - r, span, 2)
        n_per_w = n_narrow // n_wide
        w_per_g = n_wide // GROUPS
        cols = span * b_blk // w_per_g
        ordered = ordered.reshape(n_per_w, pairs_w // n_per_w, rows, w_per_g, cols)
        ladder = None
        for t in range(span):
            k = (t + r) % span
            piece = lax.dynamic_index_in_dim(ordered, k // w_per_g, 0, keepdims=False)
            piece = lax.dynamic_index_in_dim(piece, k % w_per_g, 2, keepdims=False)
            perm = []
            for gg in range(GROUPS):
                for rr in range(span):
                    for ww in range(n_wide):
                        kk = (t + rr) % span
                        dst_n = ww * n_per_w + kk // w_per_g
                        dst_w = gg * w_per_g + kk % w_per_g
                        perm.append(((gg * span + rr) * n_wide + ww, dst_n * n_wide + dst_w))
            piece = lax.ppermute(piece, ("narrow", "wide"), perm)
            ladder = piece if ladder is None else ladder + piece

        local_cols = ladder.shape[2]
        occ_ids = jnp.arange(occ_energy.shape[0], dtype=jnp.int32)
        occ_first = jnp.sum(
            jnp.where(pair_list[:, 0:1] == occ_ids[None, :], occ_energy[None, :], 0.0), axis=1
        )
        occ_second = jnp.sum(
            jnp.where(pair_list[:, 1:2] == occ_ids[None, :], occ_energy[None, :], 0.0), axis=1
        )
        vir_cols = lax.dynamic_slice_in_dim(vir_energy, w * local_cols, local_cols, 0)
        vir_rows = vir_energy[:rows]
        denominator = (
            (occ_first + occ_second)[:, None, None] - vir_rows[None, :, None] - vir_cols[None, None, :]
        )
        return ladder / denominator

    return body


def solution(mesh):
    return jax.shard_map(
        make_body(mesh.shape["narrow"], mesh.shape["wide"]),
        mesh=mesh,
        in_specs=(
            P(None, "narrow", "wide"),
            P(None, "narrow", None),
            P("narrow", "wide", None),
            P("narrow", None),
            P(),
            P(),
        ),
        out_specs=P("narrow", None, "wide"),
        check_vma=False,
    )
```

```python
import jax
import jax.numpy as jnp
from jax import lax
from jax.sharding import PartitionSpec as P

GROUPS = 2


def make_body(n_narrow, n_wide):
    span = n_narrow // GROUPS

    def body(amps, left_fit, right_fit, pair_list, occ_energy, vir_energy):
        n = lax.axis_index("narrow")
        w = lax.axis_index("wide")
        r = n % span
        g = n // span
        b_blk, d_blk, aux = right_fit.shape
        q_blk = aux // span
        rows, c_blk, _ = left_fit.shape
        pairs = amps.shape[0]
        vir_total = b_blk * n_narrow

        amps_blocks = [amps]
        for shift in range(1, n_narrow):
            perm = [(i, (i + shift) % n_narrow) for i in range(n_narrow)]
            amps_blocks.append(lax.ppermute(amps, "narrow", perm))
        amps_all = jnp.stack(amps_blocks, axis=1)

        c_sub = c_blk // n_wide
        left_part = lax.dynamic_slice_in_dim(left_fit, w * c_sub, c_sub, 1)
        left_part = left_part.reshape(rows, c_sub, span, q_blk).transpose(2, 0, 1, 3)
        left_send = jnp.concatenate([left_part] * GROUPS, axis=0)
        left_recv = lax.all_to_all(left_send, "narrow", 0, 0, tiled=True)
        left_rev = [left_recv[(n_narrow - j) % n_narrow][None] for j in range(n_narrow)]
        left_recv = lax.dynamic_slice_in_dim(
            jnp.concatenate(left_rev * 2, axis=0), n_narrow - n, n_narrow, 0
        )
        left_all = lax.all_gather(left_recv, "wide", axis=0, tiled=False)
        amps_all = amps_all.reshape(pairs, n_narrow, n_wide, c_sub, amps.shape[2])

        right_split = right_fit.reshape(b_blk, d_blk, span, q_blk)
        chunks = []
        for shift in range(span):
            dest = (r + shift) % span
            piece = lax.dynamic_index_in_dim(right_split, dest, 2, keepdims=False)
            if shift:
                perm = [
                    (gg * span + i, gg * span + (i + shift) % span)
                    for gg in range(GROUPS)
                    for i in range(span)
                ]
                piece = lax.ppermute(piece, "narrow", perm)
            chunks.append(piece)

        inter = jnp.einsum(
            "wkaiq,pkwid->padq", left_all, amps_all, preferred_element_type=jnp.float32
        ).astype(jnp.bfloat16)

        right_group = jnp.concatenate(chunks, axis=0)
        part = jnp.einsum(
            "padq,bdq->pab", inter, right_group, preferred_element_type=jnp.float32
        )
        part = lax.psum_scatter(part, "wide", scatter_dimension=0, tiled=True)
        pairs_w = part.shape[0]
        part = part.reshape(pairs_w, rows, span, b_blk)
        flipped = jnp.concatenate(
            [part[:, :, (span - k) % span : (span - k) % span + 1] for k in range(span)] * 2, axis=2
        )
        ordered = lax.dynamic_slice_in_dim(flipped, span - r, span, 2)
        n_per_w = n_narrow // n_wide
        w_per_g = n_wide // GROUPS
        cols = span * b_blk // w_per_g
        ordered = ordered.reshape(n_per_w, pairs_w // n_per_w, rows, w_per_g, cols)
        ladder = None
        for t in range(span):
            k = (t + r) % span
            piece = lax.dynamic_index_in_dim(ordered, k // w_per_g, 0, keepdims=False)
            piece = lax.dynamic_index_in_dim(piece, k % w_per_g, 2, keepdims=False)
            perm = []
            for gg in range(GROUPS):
                for rr in range(span):
                    for ww in range(n_wide):
                        kk = (t + rr) % span
                        dst_n = ww * n_per_w + kk // w_per_g
                        dst_w = gg * w_per_g + kk % w_per_g
                        perm.append(((gg * span + rr) * n_wide + ww, dst_n * n_wide + dst_w))
            piece = lax.ppermute(piece, ("narrow", "wide"), perm)
            ladder = piece if ladder is None else ladder + piece

        local_cols = ladder.shape[2]
        occ_ids = jnp.arange(occ_energy.shape[0], dtype=jnp.int32)
        occ_first = jnp.sum(
            jnp.where(pair_list[:, 0:1] == occ_ids[None, :], occ_energy[None, :], 0.0), axis=1
        )
        occ_second = jnp.sum(
            jnp.where(pair_list[:, 1:2] == occ_ids[None, :], occ_energy[None, :], 0.0), axis=1
        )
        vir_cols = lax.dynamic_slice_in_dim(vir_energy, w * local_cols, local_cols, 0)
        vir_rows = vir_energy[:rows]
        denominator = (
            (occ_first + occ_second)[:, None, None] - vir_rows[None, :, None] - vir_cols[None, None, :]
        )
        return ladder / denominator

    return body


def solution(mesh):
    return jax.shard_map(
        make_body(mesh.shape["narrow"], mesh.shape["wide"]),
        mesh=mesh,
        in_specs=(
            P(None, "narrow", "wide"),
            P(None, "narrow", None),
            P("narrow", "wide", None),
            P("narrow", None),
            P(),
            P(),
        ),
        out_specs=P("narrow", None, "wide"),
        check_vma=False,
    )
```

```python
import jax
import jax.numpy as jnp
from jax import lax
from jax.sharding import PartitionSpec as P

GROUPS = 2


def make_body(n_narrow, n_wide):
    span = n_narrow // GROUPS

    def body(amps, left_fit, right_fit, pair_list, occ_energy, vir_energy):
        n = lax.axis_index("narrow")
        w = lax.axis_index("wide")
        r = n % span
        g = n // span
        b_blk, d_blk, aux = right_fit.shape
        q_blk = aux // span
        rows, c_blk, _ = left_fit.shape
        pairs = amps.shape[0]
        vir_total = b_blk * n_narrow

        amps_blocks = [amps]
        for shift in range(1, n_narrow):
            perm = [(i, (i + shift) % n_narrow) for i in range(n_narrow)]
            amps_blocks.append(lax.ppermute(amps, "narrow", perm))
        amps_all = jnp.stack(amps_blocks, axis=1)

        c_sub = c_blk // n_wide
        left_part = lax.dynamic_slice_in_dim(left_fit, w * c_sub, c_sub, 1)
        left_part = left_part.reshape(rows, c_sub, span, q_blk).transpose(2, 3, 1, 0)
        left_send = jnp.concatenate([left_part] * GROUPS, axis=0)
        left_recv = lax.all_to_all(left_send, "narrow", 0, 0, tiled=True)
        left_rev = [left_recv[(n_narrow - j) % n_narrow][None] for j in range(n_narrow)]
        left_recv = lax.dynamic_slice_in_dim(
            jnp.concatenate(left_rev * 2, axis=0), n_narrow - n, n_narrow, 0
        )
        left_all = lax.all_gather(left_recv, "wide", axis=0, tiled=False)
        amps_all = amps_all.reshape(pairs, n_narrow, n_wide, c_sub, amps.shape[2])

        right_split = right_fit.reshape(b_blk, d_blk, span, q_blk)
        chunks = []
        for shift in range(span):
            dest = (r + shift) % span
            piece = lax.dynamic_index_in_dim(right_split, dest, 2, keepdims=False)
            if shift:
                perm = [
                    (gg * span + i, gg * span + (i + shift) % span)
                    for gg in range(GROUPS)
                    for i in range(span)
                ]
                piece = lax.ppermute(piece, "narrow", perm)
            chunks.append(piece)

        inter = jnp.einsum(
            "wkqia,pkwid->padq", left_all, amps_all, preferred_element_type=jnp.float32
        ).astype(jnp.bfloat16)

        right_group = jnp.concatenate(chunks, axis=0)
        part = jnp.einsum(
            "padq,bdq->pab", inter, right_group, preferred_element_type=jnp.float32
        )
        part = lax.psum_scatter(part, "wide", scatter_dimension=0, tiled=True)
        pairs_w = part.shape[0]
        part = part.reshape(pairs_w, rows, span, b_blk)
        flipped = jnp.concatenate(
            [part[:, :, (span - k) % span : (span - k) % span + 1] for k in range(span)] * 2, axis=2
        )
        ordered = lax.dynamic_slice_in_dim(flipped, span - r, span, 2)
        n_per_w = n_narrow // n_wide
        w_per_g = n_wide // GROUPS
        cols = span * b_blk // w_per_g
        ordered = ordered.reshape(n_per_w, pairs_w // n_per_w, rows, w_per_g, cols)
        ladder = None
        for t in range(span):
            k = (t + r) % span
            piece = lax.dynamic_index_in_dim(ordered, k // w_per_g, 0, keepdims=False)
            piece = lax.dynamic_index_in_dim(piece, k % w_per_g, 2, keepdims=False)
            perm = []
            for gg in range(GROUPS):
                for rr in range(span):
                    for ww in range(n_wide):
                        kk = (t + rr) % span
                        dst_n = ww * n_per_w + kk // w_per_g
                        dst_w = gg * w_per_g + kk % w_per_g
                        perm.append(((gg * span + rr) * n_wide + ww, dst_n * n_wide + dst_w))
            piece = lax.ppermute(piece, ("narrow", "wide"), perm)
            ladder = piece if ladder is None else ladder + piece

        local_cols = ladder.shape[2]
        occ_ids = jnp.arange(occ_energy.shape[0], dtype=jnp.int32)
        occ_first = jnp.sum(
            jnp.where(pair_list[:, 0:1] == occ_ids[None, :], occ_energy[None, :], 0.0), axis=1
        )
        occ_second = jnp.sum(
            jnp.where(pair_list[:, 1:2] == occ_ids[None, :], occ_energy[None, :], 0.0), axis=1
        )
        vir_cols = lax.dynamic_slice_in_dim(vir_energy, w * local_cols, local_cols, 0)
        vir_rows = vir_energy[:rows]
        denominator = (
            (occ_first + occ_second)[:, None, None] - vir_rows[None, :, None] - vir_cols[None, None, :]
        )
        return ladder / denominator

    return body


def solution(mesh):
    return jax.shard_map(
        make_body(mesh.shape["narrow"], mesh.shape["wide"]),
        mesh=mesh,
        in_specs=(
            P(None, "narrow", "wide"),
            P(None, "narrow", None),
            P("narrow", "wide", None),
            P("narrow", None),
            P(),
            P(),
        ),
        out_specs=P("narrow", None, "wide"),
        check_vma=False,
    )
```

```python
import jax
import jax.numpy as jnp
from jax import lax
from jax.sharding import PartitionSpec as P

GROUPS = 2


def make_body(n_narrow, n_wide):
    span = n_narrow // GROUPS

    def body(amps, left_fit, right_fit, pair_list, occ_energy, vir_energy):
        n = lax.axis_index("narrow")
        w = lax.axis_index("wide")
        r = n % span
        g = n // span
        b_blk, d_blk, aux = right_fit.shape
        q_blk = aux // span
        rows, c_blk, _ = left_fit.shape
        pairs = amps.shape[0]
        vir_total = b_blk * n_narrow

        amps_blocks = [amps]
        for shift in range(1, n_narrow):
            perm = [(i, (i + shift) % n_narrow) for i in range(n_narrow)]
            amps_blocks.append(lax.ppermute(amps, "narrow", perm))
        amps_all = jnp.stack(amps_blocks, axis=1)

        c_sub = c_blk // n_wide
        left_part = lax.dynamic_slice_in_dim(left_fit, w * c_sub, c_sub, 1)
        left_part = left_part.reshape(rows, c_sub, span, q_blk).transpose(2, 3, 1, 0)
        left_send = jnp.concatenate([left_part] * GROUPS, axis=0)
        left_recv = lax.all_to_all(left_send, "narrow", 0, 0, tiled=True)
        left_rev = [left_recv[(n_narrow - j) % n_narrow][None] for j in range(n_narrow)]
        left_recv = lax.dynamic_slice_in_dim(
            jnp.concatenate(left_rev * 2, axis=0), n_narrow - n, n_narrow, 0
        )
        left_all = lax.all_gather(left_recv, "wide", axis=0, tiled=False)
        amps_all = amps_all.reshape(pairs, n_narrow, n_wide, c_sub, amps.shape[2])

        right_split = right_fit.reshape(b_blk, d_blk, span, q_blk)
        chunks = []
        for shift in range(span):
            dest = (r + shift) % span
            piece = lax.dynamic_index_in_dim(right_split, dest, 2, keepdims=False)
            if shift:
                perm = [
                    (gg * span + i, gg * span + (i + shift) % span)
                    for gg in range(GROUPS)
                    for i in range(span)
                ]
                piece = lax.ppermute(piece, "narrow", perm)
            chunks.append(piece)

        inter = jnp.einsum(
            "wkqia,pkwid->padq", left_all, amps_all, preferred_element_type=jnp.float32
        ).astype(jnp.bfloat16)

        right_group = jnp.concatenate(chunks, axis=0)
        part = jnp.einsum(
            "padq,bdq->pab", inter, right_group, preferred_element_type=jnp.float32
        )
        pairs_w = pairs // n_wide
        part = part.reshape(n_wide, pairs_w, rows, span * b_blk)
        summed = lax.dynamic_index_in_dim(part, w, 0, keepdims=False)
        for shift in range(1, n_wide):
            perm = [(i, (i + shift) % n_wide) for i in range(n_wide)]
            piece = lax.dynamic_index_in_dim(part, (w + shift) % n_wide, 0, keepdims=False)
            summed = summed + lax.ppermute(piece, "wide", perm)
        part = summed
        part = part.reshape(pairs_w, rows, span, b_blk)
        flipped = jnp.concatenate(
            [part[:, :, (span - k) % span : (span - k) % span + 1] for k in range(span)] * 2, axis=2
        )
        ordered = lax.dynamic_slice_in_dim(flipped, span - r, span, 2)
        n_per_w = n_narrow // n_wide
        w_per_g = n_wide // GROUPS
        cols = span * b_blk // w_per_g
        ordered = ordered.reshape(n_per_w, pairs_w // n_per_w, rows, w_per_g, cols)
        ladder = None
        for t in range(span):
            k = (t + r) % span
            piece = lax.dynamic_index_in_dim(ordered, k // w_per_g, 0, keepdims=False)
            piece = lax.dynamic_index_in_dim(piece, k % w_per_g, 2, keepdims=False)
            perm = []
            for gg in range(GROUPS):
                for rr in range(span):
                    for ww in range(n_wide):
                        kk = (t + rr) % span
                        dst_n = ww * n_per_w + kk // w_per_g
                        dst_w = gg * w_per_g + kk % w_per_g
                        perm.append(((gg * span + rr) * n_wide + ww, dst_n * n_wide + dst_w))
            piece = lax.ppermute(piece, ("narrow", "wide"), perm)
            ladder = piece if ladder is None else ladder + piece

        local_cols = ladder.shape[2]
        occ_ids = jnp.arange(occ_energy.shape[0], dtype=jnp.int32)
        occ_first = jnp.sum(
            jnp.where(pair_list[:, 0:1] == occ_ids[None, :], occ_energy[None, :], 0.0), axis=1
        )
        occ_second = jnp.sum(
            jnp.where(pair_list[:, 1:2] == occ_ids[None, :], occ_energy[None, :], 0.0), axis=1
        )
        vir_cols = lax.dynamic_slice_in_dim(vir_energy, w * local_cols, local_cols, 0)
        vir_rows = vir_energy[:rows]
        denominator = (
            (occ_first + occ_second)[:, None, None] - vir_rows[None, :, None] - vir_cols[None, None, :]
        )
        return ladder / denominator

    return body


def solution(mesh):
    return jax.shard_map(
        make_body(mesh.shape["narrow"], mesh.shape["wide"]),
        mesh=mesh,
        in_specs=(
            P(None, "narrow", "wide"),
            P(None, "narrow", None),
            P("narrow", "wide", None),
            P("narrow", None),
            P(),
            P(),
        ),
        out_specs=P("narrow", None, "wide"),
        check_vma=False,
    )
```

```python
import jax
import jax.numpy as jnp
from jax import lax
from jax.sharding import PartitionSpec as P

GROUPS = 2


def make_body(n_narrow, n_wide):
    span = n_narrow // GROUPS

    def body(amps, left_fit, right_fit, pair_list, occ_energy, vir_energy):
        n = lax.axis_index("narrow")
        w = lax.axis_index("wide")
        r = n % span
        g = n // span
        b_blk, d_blk, aux = right_fit.shape
        q_blk = aux // span
        rows, c_blk, _ = left_fit.shape
        pairs = amps.shape[0]
        vir_total = b_blk * n_narrow

        right_split = right_fit.reshape(b_blk, d_blk, span, q_blk)
        amps_size = amps.size

        def perm_of(shift, step):
            return [
                (gg * span + i, ((gg + step) % GROUPS) * span + (i + shift) % span)
                for gg in range(GROUPS)
                for i in range(span)
            ]

        amps_blocks = []
        chunks = []
        for step in range(GROUPS):
            for shift in range(span):
                if step == 0 and shift == 0:
                    amps_blocks.append(amps)
                    chunks.append(lax.dynamic_index_in_dim(right_split, r, 2, keepdims=False))
                elif step == 0:
                    piece = lax.dynamic_index_in_dim(right_split, (r + shift) % span, 2, keepdims=False)
                    both = jnp.concatenate([amps.reshape(-1), piece.reshape(-1)])
                    both = lax.ppermute(both, "narrow", perm_of(shift, 0))
                    amps_blocks.append(both[:amps_size].reshape(amps.shape))
                    chunks.append(both[amps_size:].reshape(piece.shape))
                else:
                    amps_blocks.append(lax.ppermute(amps, "narrow", perm_of(shift, step)))
        amps_all = jnp.stack(amps_blocks, axis=1)

        def rotate_back(x, by, size, axis):
            rev = [lax.slice_in_dim(x, (size - j) % size, (size - j) % size + 1, axis=axis) for j in range(size)]
            return lax.dynamic_slice_in_dim(jnp.concatenate(rev * 2, axis=axis), size - by, size, axis)

        c_sub = c_blk // n_wide
        left_part = lax.dynamic_slice_in_dim(left_fit, w * c_sub, c_sub, 1)
        left_part = left_part.reshape(rows, c_sub, span, q_blk).transpose(2, 3, 1, 0)
        left_send = jnp.concatenate([left_part] * GROUPS, axis=0)
        left_recv = lax.all_to_all(left_send, "narrow", 0, 0, tiled=True)
        left_recv = left_recv.reshape((GROUPS, span) + left_recv.shape[1:])
        left_recv = rotate_back(rotate_back(left_recv, r, span, 1), g, GROUPS, 0)
        left_recv = left_recv.reshape((n_narrow,) + left_recv.shape[2:])
        left_all = lax.all_gather(left_recv, "wide", axis=0, tiled=False)
        amps_all = amps_all.reshape(pairs, n_narrow, n_wide, c_sub, amps.shape[2])

        inter = jnp.einsum(
            "wkqia,pkwid->padq", left_all, amps_all, preferred_element_type=jnp.float32
        ).astype(jnp.bfloat16)

        right_group = jnp.concatenate(chunks, axis=0)
        part = jnp.einsum(
            "padq,bdq->pab", inter, right_group, preferred_element_type=jnp.float32
        )
        pairs_w = pairs // n_wide
        part = part.reshape(n_wide, pairs_w, rows, span * b_blk)
        summed = lax.dynamic_index_in_dim(part, w, 0, keepdims=False)
        for shift in range(1, n_wide):
            perm = [(i, (i + shift) % n_wide) for i in range(n_wide)]
            piece = lax.dynamic_index_in_dim(part, (w + shift) % n_wide, 0, keepdims=False)
            summed = summed + lax.ppermute(piece, "wide", perm)
        part = summed
        part = part.reshape(pairs_w, rows, span, b_blk)
        flipped = jnp.concatenate(
            [part[:, :, (span - k) % span : (span - k) % span + 1] for k in range(span)] * 2, axis=2
        )
        ordered = lax.dynamic_slice_in_dim(flipped, span - r, span, 2)
        n_per_w = n_narrow // n_wide
        w_per_g = n_wide // GROUPS
        cols = span * b_blk // w_per_g
        ordered = ordered.reshape(n_per_w, pairs_w // n_per_w, rows, w_per_g, cols)
        ladder = None
        for t in range(span):
            k = (t + r) % span
            piece = lax.dynamic_index_in_dim(ordered, k // w_per_g, 0, keepdims=False)
            piece = lax.dynamic_index_in_dim(piece, k % w_per_g, 2, keepdims=False)
            perm = []
            for gg in range(GROUPS):
                for rr in range(span):
                    for ww in range(n_wide):
                        kk = (t + rr) % span
                        dst_n = ww * n_per_w + kk // w_per_g
                        dst_w = gg * w_per_g + kk % w_per_g
                        perm.append(((gg * span + rr) * n_wide + ww, dst_n * n_wide + dst_w))
            piece = lax.ppermute(piece, ("narrow", "wide"), perm)
            ladder = piece if ladder is None else ladder + piece

        local_cols = ladder.shape[2]
        occ_ids = jnp.arange(occ_energy.shape[0], dtype=jnp.int32)
        occ_first = jnp.sum(
            jnp.where(pair_list[:, 0:1] == occ_ids[None, :], occ_energy[None, :], 0.0), axis=1
        )
        occ_second = jnp.sum(
            jnp.where(pair_list[:, 1:2] == occ_ids[None, :], occ_energy[None, :], 0.0), axis=1
        )
        vir_cols = lax.dynamic_slice_in_dim(vir_energy, w * local_cols, local_cols, 0)
        vir_rows = vir_energy[:rows]
        denominator = (
            (occ_first + occ_second)[:, None, None] - vir_rows[None, :, None] - vir_cols[None, None, :]
        )
        return ladder / denominator

    return body


def solution(mesh):
    return jax.shard_map(
        make_body(mesh.shape["narrow"], mesh.shape["wide"]),
        mesh=mesh,
        in_specs=(
            P(None, "narrow", "wide"),
            P(None, "narrow", None),
            P("narrow", "wide", None),
            P("narrow", None),
            P(),
            P(),
        ),
        out_specs=P("narrow", None, "wide"),
        check_vma=False,
    )
```

```python
import jax
import jax.numpy as jnp
from jax import lax
from jax.sharding import PartitionSpec as P

GROUPS = 2


def make_body(n_narrow, n_wide):
    span = n_narrow // GROUPS

    def body(amps, left_fit, right_fit, pair_list, occ_energy, vir_energy):
        n = lax.axis_index("narrow")
        w = lax.axis_index("wide")
        r = n % span
        g = n // span
        b_blk, d_blk, aux = right_fit.shape
        q_blk = aux // span
        rows, c_blk, _ = left_fit.shape
        pairs = amps.shape[0]
        vir_total = b_blk * n_narrow

        c_sub = c_blk // n_wide
        left_part = lax.dynamic_slice_in_dim(left_fit, w * c_sub, c_sub, 1)
        left_part = left_part.reshape(rows, c_sub, span, q_blk).transpose(2, 3, 1, 0)
        left_piece = left_part[0].size
        left_send = jnp.concatenate([left_part.reshape(span, left_piece)] * GROUPS, axis=0)
        amps_send = jnp.broadcast_to(amps.reshape(1, -1), (n_narrow, amps.size))
        both = lax.all_to_all(
            jnp.concatenate([left_send, amps_send], axis=1), "narrow", 0, 0, tiled=True
        )
        left_recv = both[:, :left_piece].reshape((n_narrow,) + left_part.shape[1:])
        amps_all = both[:, left_piece:].reshape(n_narrow, pairs, n_wide, c_sub, amps.shape[2])
        left_all = lax.all_gather(left_recv, "wide", axis=0, tiled=False)

        right_split = right_fit.reshape(b_blk, d_blk, span, q_blk)
        chunks = []
        for shift in range(span):
            dest = (r + shift) % span
            piece = lax.dynamic_index_in_dim(right_split, dest, 2, keepdims=False)
            if shift:
                perm = [
                    (gg * span + i, gg * span + (i + shift) % span)
                    for gg in range(GROUPS)
                    for i in range(span)
                ]
                piece = lax.ppermute(piece, "narrow", perm)
            chunks.append(piece)

        inter = jnp.einsum(
            "wkqia,kpwid->padq", left_all, amps_all, preferred_element_type=jnp.float32
        ).astype(jnp.bfloat16)

        right_group = jnp.concatenate(chunks, axis=0)
        part = jnp.einsum(
            "padq,bdq->pab", inter, right_group, preferred_element_type=jnp.float32
        )
        pairs_w = pairs // n_wide
        part = part.reshape(n_wide, pairs_w, rows, span * b_blk)
        summed = lax.dynamic_index_in_dim(part, w, 0, keepdims=False)
        for shift in range(1, n_wide):
            perm = [(i, (i + shift) % n_wide) for i in range(n_wide)]
            piece = lax.dynamic_index_in_dim(part, (w + shift) % n_wide, 0, keepdims=False)
            summed = summed + lax.ppermute(piece, "wide", perm)
        part = summed
        part = part.reshape(pairs_w, rows, span, b_blk)
        flipped = jnp.concatenate(
            [part[:, :, (span - k) % span : (span - k) % span + 1] for k in range(span)] * 2, axis=2
        )
        ordered = lax.dynamic_slice_in_dim(flipped, span - r, span, 2)
        n_per_w = n_narrow // n_wide
        w_per_g = n_wide // GROUPS
        cols = span * b_blk // w_per_g
        ordered = ordered.reshape(n_per_w, pairs_w // n_per_w, rows, w_per_g, cols)
        ladder = None
        for t in range(span):
            k = (t + r) % span
            piece = lax.dynamic_index_in_dim(ordered, k // w_per_g, 0, keepdims=False)
            piece = lax.dynamic_index_in_dim(piece, k % w_per_g, 2, keepdims=False)
            perm = []
            for gg in range(GROUPS):
                for rr in range(span):
                    for ww in range(n_wide):
                        kk = (t + rr) % span
                        dst_n = ww * n_per_w + kk // w_per_g
                        dst_w = gg * w_per_g + kk % w_per_g
                        perm.append(((gg * span + rr) * n_wide + ww, dst_n * n_wide + dst_w))
            piece = lax.ppermute(piece, ("narrow", "wide"), perm)
            ladder = piece if ladder is None else ladder + piece

        local_cols = ladder.shape[2]
        occ_ids = jnp.arange(occ_energy.shape[0], dtype=jnp.int32)
        occ_first = jnp.sum(
            jnp.where(pair_list[:, 0:1] == occ_ids[None, :], occ_energy[None, :], 0.0), axis=1
        )
        occ_second = jnp.sum(
            jnp.where(pair_list[:, 1:2] == occ_ids[None, :], occ_energy[None, :], 0.0), axis=1
        )
        vir_cols = lax.dynamic_slice_in_dim(vir_energy, w * local_cols, local_cols, 0)
        vir_rows = vir_energy[:rows]
        denominator = (
            (occ_first + occ_second)[:, None, None] - vir_rows[None, :, None] - vir_cols[None, None, :]
        )
        return ladder / denominator

    return body


def solution(mesh):
    return jax.shard_map(
        make_body(mesh.shape["narrow"], mesh.shape["wide"]),
        mesh=mesh,
        in_specs=(
            P(None, "narrow", "wide"),
            P(None, "narrow", None),
            P("narrow", "wide", None),
            P("narrow", None),
            P(),
            P(),
        ),
        out_specs=P("narrow", None, "wide"),
        check_vma=False,
    )
```

```python
import jax
import jax.numpy as jnp
from jax import lax
from jax.sharding import PartitionSpec as P

GROUPS = 2


def make_body(n_narrow, n_wide):
    span = n_narrow // GROUPS

    def body(amps, left_fit, right_fit, pair_list, occ_energy, vir_energy):
        n = lax.axis_index("narrow")
        w = lax.axis_index("wide")
        r = n % span
        g = n // span
        b_blk, d_blk, aux = right_fit.shape
        q_blk = aux // span
        rows, c_blk, _ = left_fit.shape
        pairs = amps.shape[0]
        vir_total = b_blk * n_narrow

        amps_all = lax.all_gather(amps, "narrow", axis=1, tiled=True)

        c_sub = c_blk // n_wide
        left_part = lax.dynamic_slice_in_dim(left_fit, w * c_sub, c_sub, 1)
        left_part = left_part.reshape(rows, c_sub, span, q_blk).transpose(2, 3, 1, 0)
        left_send = jnp.concatenate([left_part] * GROUPS, axis=0)
        left_recv = lax.all_to_all(left_send, "narrow", 0, 0, tiled=True)
        left_slots = [left_recv]
        for shift in range(1, n_wide):
            perm = [(i, (i + shift) % n_wide) for i in range(n_wide)]
            left_slots.append(lax.ppermute(left_recv, "wide", perm))
        left_all = jnp.stack(left_slots, axis=0)
        amps_all = amps_all.reshape(pairs, n_narrow, n_wide, c_sub, amps.shape[2])
        amps_rev = [
            lax.slice_in_dim(amps_all, (n_wide - j) % n_wide, (n_wide - j) % n_wide + 1, axis=2)
            for j in range(n_wide)
        ]
        amps_all = lax.dynamic_slice_in_dim(
            jnp.concatenate(amps_rev * 2, axis=2), n_wide - w, n_wide, 2
        )

        right_split = right_fit.reshape(b_blk, d_blk, span, q_blk)
        chunks = []
        for shift in range(span):
            dest = (r + shift) % span
            piece = lax.dynamic_index_in_dim(right_split, dest, 2, keepdims=False)
            if shift:
                perm = [
                    (gg * span + i, gg * span + (i + shift) % span)
                    for gg in range(GROUPS)
                    for i in range(span)
                ]
                piece = lax.ppermute(piece, "narrow", perm)
            chunks.append(piece)

        inter = jnp.einsum(
            "wkqia,pkwid->padq", left_all, amps_all, preferred_element_type=jnp.float32
        ).astype(jnp.bfloat16)

        right_group = jnp.concatenate(chunks, axis=0)
        part = jnp.einsum(
            "padq,bdq->pab", inter, right_group, preferred_element_type=jnp.float32
        )
        pairs_w = pairs // n_wide
        part = part.reshape(n_wide, pairs_w, rows, span * b_blk)
        summed = lax.dynamic_index_in_dim(part, w, 0, keepdims=False)
        for shift in range(1, n_wide):
            perm = [(i, (i + shift) % n_wide) for i in range(n_wide)]
            piece = lax.dynamic_index_in_dim(part, (w + shift) % n_wide, 0, keepdims=False)
            summed = summed + lax.ppermute(piece, "wide", perm)
        part = summed
        part = part.reshape(pairs_w, rows, span, b_blk)
        flipped = jnp.concatenate(
            [part[:, :, (span - k) % span : (span - k) % span + 1] for k in range(span)] * 2, axis=2
        )
        ordered = lax.dynamic_slice_in_dim(flipped, span - r, span, 2)
        n_per_w = n_narrow // n_wide
        w_per_g = n_wide // GROUPS
        cols = span * b_blk // w_per_g
        ordered = ordered.reshape(n_per_w, pairs_w // n_per_w, rows, w_per_g, cols)
        ladder = None
        for t in range(span):
            k = (t + r) % span
            piece = lax.dynamic_index_in_dim(ordered, k // w_per_g, 0, keepdims=False)
            piece = lax.dynamic_index_in_dim(piece, k % w_per_g, 2, keepdims=False)
            perm = []
            for gg in range(GROUPS):
                for rr in range(span):
                    for ww in range(n_wide):
                        kk = (t + rr) % span
                        dst_n = ww * n_per_w + kk // w_per_g
                        dst_w = gg * w_per_g + kk % w_per_g
                        perm.append(((gg * span + rr) * n_wide + ww, dst_n * n_wide + dst_w))
            piece = lax.ppermute(piece, ("narrow", "wide"), perm)
            ladder = piece if ladder is None else ladder + piece

        local_cols = ladder.shape[2]
        occ_ids = jnp.arange(occ_energy.shape[0], dtype=jnp.int32)
        occ_first = jnp.sum(
            jnp.where(pair_list[:, 0:1] == occ_ids[None, :], occ_energy[None, :], 0.0), axis=1
        )
        occ_second = jnp.sum(
            jnp.where(pair_list[:, 1:2] == occ_ids[None, :], occ_energy[None, :], 0.0), axis=1
        )
        vir_cols = lax.dynamic_slice_in_dim(vir_energy, w * local_cols, local_cols, 0)
        vir_rows = vir_energy[:rows]
        denominator = (
            (occ_first + occ_second)[:, None, None] - vir_rows[None, :, None] - vir_cols[None, None, :]
        )
        return ladder / denominator

    return body


def solution(mesh):
    return jax.shard_map(
        make_body(mesh.shape["narrow"], mesh.shape["wide"]),
        mesh=mesh,
        in_specs=(
            P(None, "narrow", "wide"),
            P(None, "narrow", None),
            P("narrow", "wide", None),
            P("narrow", None),
            P(),
            P(),
        ),
        out_specs=P("narrow", None, "wide"),
        check_vma=False,
    )
```

```python
import jax
import jax.numpy as jnp
from jax import lax
from jax.sharding import PartitionSpec as P

GROUPS = 2


def make_body(n_narrow, n_wide):
    span = n_narrow // GROUPS

    def body(amps, left_fit, right_fit, pair_list, occ_energy, vir_energy):
        n = lax.axis_index("narrow")
        w = lax.axis_index("wide")
        r = n % span
        g = n // span
        b_blk, d_blk, aux = right_fit.shape
        q_blk = aux // span
        rows, c_blk, _ = left_fit.shape
        pairs = amps.shape[0]
        vir_total = b_blk * n_narrow

        c_sub = c_blk // n_wide
        left_part = lax.dynamic_slice_in_dim(left_fit, w * c_sub, c_sub, 1)
        left_part = left_part.reshape(rows, c_sub, span, q_blk).transpose(2, 3, 1, 0)
        left_send = jnp.concatenate([left_part] * GROUPS, axis=0)
        left_recv = lax.all_to_all(left_send, "narrow", 0, 0, tiled=True)
        amps, left_recv = lax.optimization_barrier((amps, left_recv))
        amps_blocks = [amps]
        for shift in range(1, n_narrow):
            perm = [(i, (i + shift) % n_narrow) for i in range(n_narrow)]
            amps_blocks.append(lax.ppermute(amps, "narrow", perm))
        amps_all = jnp.stack(amps_blocks, axis=1)

        left_rev = [left_recv[(n_narrow - j) % n_narrow][None] for j in range(n_narrow)]
        left_recv = lax.dynamic_slice_in_dim(
            jnp.concatenate(left_rev * 2, axis=0), n_narrow - n, n_narrow, 0
        )
        left_all = lax.all_gather(left_recv, "wide", axis=0, tiled=False)
        amps_all = amps_all.reshape(pairs, n_narrow, n_wide, c_sub, amps.shape[2])

        right_split = right_fit.reshape(b_blk, d_blk, span, q_blk)
        chunks = []
        for shift in range(span):
            dest = (r + shift) % span
            piece = lax.dynamic_index_in_dim(right_split, dest, 2, keepdims=False)
            if shift:
                perm = [
                    (gg * span + i, gg * span + (i + shift) % span)
                    for gg in range(GROUPS)
                    for i in range(span)
                ]
                piece = lax.ppermute(piece, "narrow", perm)
            chunks.append(piece)

        inter = jnp.einsum(
            "wkqia,pkwid->padq", left_all, amps_all, preferred_element_type=jnp.float32
        ).astype(jnp.bfloat16)

        right_group = jnp.concatenate(chunks, axis=0)
        part = jnp.einsum(
            "padq,bdq->pab", inter, right_group, preferred_element_type=jnp.float32
        )
        pairs_w = pairs // n_wide
        part = part.reshape(n_wide, pairs_w, rows, span * b_blk)
        summed = lax.dynamic_index_in_dim(part, w, 0, keepdims=False)
        for shift in range(1, n_wide):
            perm = [(i, (i + shift) % n_wide) for i in range(n_wide)]
            piece = lax.dynamic_index_in_dim(part, (w + shift) % n_wide, 0, keepdims=False)
            summed = summed + lax.ppermute(piece, "wide", perm)
        part = summed
        part = part.reshape(pairs_w, rows, span, b_blk)
        flipped = jnp.concatenate(
            [part[:, :, (span - k) % span : (span - k) % span + 1] for k in range(span)] * 2, axis=2
        )
        ordered = lax.dynamic_slice_in_dim(flipped, span - r, span, 2)
        n_per_w = n_narrow // n_wide
        w_per_g = n_wide // GROUPS
        cols = span * b_blk // w_per_g
        ordered = ordered.reshape(n_per_w, pairs_w // n_per_w, rows, w_per_g, cols)
        ladder = None
        for t in range(span):
            k = (t + r) % span
            piece = lax.dynamic_index_in_dim(ordered, k // w_per_g, 0, keepdims=False)
            piece = lax.dynamic_index_in_dim(piece, k % w_per_g, 2, keepdims=False)
            perm = []
            for gg in range(GROUPS):
                for rr in range(span):
                    for ww in range(n_wide):
                        kk = (t + rr) % span
                        dst_n = ww * n_per_w + kk // w_per_g
                        dst_w = gg * w_per_g + kk % w_per_g
                        perm.append(((gg * span + rr) * n_wide + ww, dst_n * n_wide + dst_w))
            piece = lax.ppermute(piece, ("narrow", "wide"), perm)
            ladder = piece if ladder is None else ladder + piece

        local_cols = ladder.shape[2]
        occ_ids = jnp.arange(occ_energy.shape[0], dtype=jnp.int32)
        occ_first = jnp.sum(
            jnp.where(pair_list[:, 0:1] == occ_ids[None, :], occ_energy[None, :], 0.0), axis=1
        )
        occ_second = jnp.sum(
            jnp.where(pair_list[:, 1:2] == occ_ids[None, :], occ_energy[None, :], 0.0), axis=1
        )
        vir_cols = lax.dynamic_slice_in_dim(vir_energy, w * local_cols, local_cols, 0)
        vir_rows = vir_energy[:rows]
        denominator = (
            (occ_first + occ_second)[:, None, None] - vir_rows[None, :, None] - vir_cols[None, None, :]
        )
        return ladder / denominator

    return body


def solution(mesh):
    return jax.shard_map(
        make_body(mesh.shape["narrow"], mesh.shape["wide"]),
        mesh=mesh,
        in_specs=(
            P(None, "narrow", "wide"),
            P(None, "narrow", None),
            P("narrow", "wide", None),
            P("narrow", None),
            P(),
            P(),
        ),
        out_specs=P("narrow", None, "wide"),
        check_vma=False,
    )
```

```python
import jax
import jax.numpy as jnp
from jax import lax
from jax.sharding import PartitionSpec as P

GROUPS = 2


def make_body(n_narrow, n_wide):
    span = n_narrow // GROUPS

    def body(amps, left_fit, right_fit, pair_list, occ_energy, vir_energy):
        n = lax.axis_index("narrow")
        w = lax.axis_index("wide")
        r = n % span
        g = n // span
        b_blk, d_blk, aux = right_fit.shape
        q_blk = aux // span
        rows, c_blk, _ = left_fit.shape
        pairs = amps.shape[0]
        vir_total = b_blk * n_narrow

        def perm_of(shift, step):
            return [
                (gg * span + i, ((gg + step) % GROUPS) * span + (i + shift) % span)
                for gg in range(GROUPS)
                for i in range(span)
            ]

        own_set = [amps] + [lax.ppermute(amps, "narrow", perm_of(0, step)) for step in range(1, GROUPS)]
        group_set = jnp.stack(own_set, axis=0)
        shifted_sets = [group_set] + [
            lax.ppermute(group_set, "narrow", perm_of(shift, 0)) for shift in range(1, span)
        ]
        amps_all = jnp.stack(shifted_sets, axis=1)

        def rotate_back(x, by, size, axis):
            rev = [lax.slice_in_dim(x, (size - j) % size, (size - j) % size + 1, axis=axis) for j in range(size)]
            return lax.dynamic_slice_in_dim(jnp.concatenate(rev * 2, axis=axis), size - by, size, axis)

        c_sub = c_blk // n_wide
        left_part = lax.dynamic_slice_in_dim(left_fit, w * c_sub, c_sub, 1)
        left_part = left_part.reshape(rows, c_sub, span, q_blk).transpose(2, 3, 1, 0)
        left_send = jnp.concatenate([left_part] * GROUPS, axis=0)
        left_recv = lax.all_to_all(left_send, "narrow", 0, 0, tiled=True)
        left_recv = left_recv.reshape((GROUPS, span) + left_recv.shape[1:])
        left_recv = rotate_back(rotate_back(left_recv, r, span, 1), g, GROUPS, 0)
        left_recv = left_recv.reshape((n_narrow,) + left_recv.shape[2:])
        left_all = lax.all_gather(left_recv, "wide", axis=0, tiled=False)
        amps_all = amps_all.reshape(n_narrow, pairs, n_wide, c_sub, amps.shape[2])

        right_split = right_fit.reshape(b_blk, d_blk, span, q_blk)
        chunks = []
        for shift in range(span):
            dest = (r + shift) % span
            piece = lax.dynamic_index_in_dim(right_split, dest, 2, keepdims=False)
            if shift:
                perm = [
                    (gg * span + i, gg * span + (i + shift) % span)
                    for gg in range(GROUPS)
                    for i in range(span)
                ]
                piece = lax.ppermute(piece, "narrow", perm)
            chunks.append(piece)

        inter = jnp.einsum(
            "wkqia,kpwid->padq", left_all, amps_all, preferred_element_type=jnp.float32
        ).astype(jnp.bfloat16)

        right_group = jnp.concatenate(chunks, axis=0)
        part = jnp.einsum(
            "padq,bdq->pab", inter, right_group, preferred_element_type=jnp.float32
        )
        pairs_w = pairs // n_wide
        part = part.reshape(n_wide, pairs_w, rows, span * b_blk)
        summed = lax.dynamic_index_in_dim(part, w, 0, keepdims=False)
        for shift in range(1, n_wide):
            perm = [(i, (i + shift) % n_wide) for i in range(n_wide)]
            piece = lax.dynamic_index_in_dim(part, (w + shift) % n_wide, 0, keepdims=False)
            summed = summed + lax.ppermute(piece, "wide", perm)
        part = summed
        part = part.reshape(pairs_w, rows, span, b_blk)
        flipped = jnp.concatenate(
            [part[:, :, (span - k) % span : (span - k) % span + 1] for k in range(span)] * 2, axis=2
        )
        ordered = lax.dynamic_slice_in_dim(flipped, span - r, span, 2)
        n_per_w = n_narrow // n_wide
        w_per_g = n_wide // GROUPS
        cols = span * b_blk // w_per_g
        ordered = ordered.reshape(n_per_w, pairs_w // n_per_w, rows, w_per_g, cols)
        ladder = None
        for t in range(span):
            k = (t + r) % span
            piece = lax.dynamic_index_in_dim(ordered, k // w_per_g, 0, keepdims=False)
            piece = lax.dynamic_index_in_dim(piece, k % w_per_g, 2, keepdims=False)
            perm = []
            for gg in range(GROUPS):
                for rr in range(span):
                    for ww in range(n_wide):
                        kk = (t + rr) % span
                        dst_n = ww * n_per_w + kk // w_per_g
                        dst_w = gg * w_per_g + kk % w_per_g
                        perm.append(((gg * span + rr) * n_wide + ww, dst_n * n_wide + dst_w))
            piece = lax.ppermute(piece, ("narrow", "wide"), perm)
            ladder = piece if ladder is None else ladder + piece

        local_cols = ladder.shape[2]
        occ_ids = jnp.arange(occ_energy.shape[0], dtype=jnp.int32)
        occ_first = jnp.sum(
            jnp.where(pair_list[:, 0:1] == occ_ids[None, :], occ_energy[None, :], 0.0), axis=1
        )
        occ_second = jnp.sum(
            jnp.where(pair_list[:, 1:2] == occ_ids[None, :], occ_energy[None, :], 0.0), axis=1
        )
        vir_cols = lax.dynamic_slice_in_dim(vir_energy, w * local_cols, local_cols, 0)
        vir_rows = vir_energy[:rows]
        denominator = (
            (occ_first + occ_second)[:, None, None] - vir_rows[None, :, None] - vir_cols[None, None, :]
        )
        return ladder / denominator

    return body


def solution(mesh):
    return jax.shard_map(
        make_body(mesh.shape["narrow"], mesh.shape["wide"]),
        mesh=mesh,
        in_specs=(
            P(None, "narrow", "wide"),
            P(None, "narrow", None),
            P("narrow", "wide", None),
            P("narrow", None),
            P(),
            P(),
        ),
        out_specs=P("narrow", None, "wide"),
        check_vma=False,
    )
```

```python
import jax
import jax.numpy as jnp
from jax import lax
from jax.sharding import PartitionSpec as P

GROUPS = 2


def make_body(n_narrow, n_wide):
    span = n_narrow // GROUPS

    def body(amps, left_fit, right_fit, pair_list, occ_energy, vir_energy):
        n = lax.axis_index("narrow")
        w = lax.axis_index("wide")
        r = n % span
        g = n // span
        b_blk, d_blk, aux = right_fit.shape
        q_blk = aux // span
        rows, c_blk, _ = left_fit.shape
        pairs = amps.shape[0]
        vir_total = b_blk * n_narrow

        def perm_of(shift, step):
            return [
                (gg * span + i, ((gg + step) % GROUPS) * span + (i + shift) % span)
                for gg in range(GROUPS)
                for i in range(span)
            ]

        own_set = [amps] + [lax.ppermute(amps, "narrow", perm_of(0, step)) for step in range(1, GROUPS)]
        group_set = jnp.stack(own_set, axis=0)
        shifted_sets = [group_set] + [
            lax.ppermute(group_set, "narrow", perm_of(shift, 0)) for shift in range(1, span)
        ]
        amps_all = jnp.stack(shifted_sets, axis=1)

        def rotate_back(x, by, size, axis):
            rev = [lax.slice_in_dim(x, (size - j) % size, (size - j) % size + 1, axis=axis) for j in range(size)]
            return lax.dynamic_slice_in_dim(jnp.concatenate(rev * 2, axis=axis), size - by, size, axis)

        c_sub = c_blk // n_wide
        left_part = lax.dynamic_slice_in_dim(left_fit, w * c_sub, c_sub, 1)
        left_part = left_part.reshape(rows, c_sub, span, q_blk).transpose(2, 3, 1, 0)
        left_send = jnp.concatenate([left_part] * GROUPS, axis=0)
        left_recv = lax.all_to_all(left_send, "narrow", 0, 0, tiled=True)
        left_recv = left_recv.reshape((GROUPS, span) + left_recv.shape[1:])
        left_recv = rotate_back(rotate_back(left_recv, r, span, 1), g, GROUPS, 0)
        left_recv = left_recv.reshape((n_narrow,) + left_recv.shape[2:])
        left_all = lax.all_gather(left_recv, "wide", axis=0, tiled=False)
        amps_all = amps_all.reshape(n_narrow, pairs, n_wide, c_sub, amps.shape[2])

        right_split = right_fit.reshape(b_blk, d_blk, span, q_blk)
        chunks = []
        for shift in range(span):
            dest = (r + shift) % span
            piece = lax.select_n(dest, *[right_split[:, :, j] for j in range(span)])
            if shift:
                perm = [
                    (gg * span + i, gg * span + (i + shift) % span)
                    for gg in range(GROUPS)
                    for i in range(span)
                ]
                piece = lax.ppermute(piece, "narrow", perm)
            chunks.append(piece)

        inter = jnp.einsum(
            "wkqia,kpwid->padq", left_all, amps_all, preferred_element_type=jnp.float32
        ).astype(jnp.bfloat16)

        right_group = jnp.concatenate(chunks, axis=0)
        part = jnp.einsum(
            "padq,bdq->pab", inter, right_group, preferred_element_type=jnp.float32
        )
        pairs_w = pairs // n_wide
        part = part.reshape(n_wide, pairs_w, rows, span * b_blk)
        summed = lax.dynamic_index_in_dim(part, w, 0, keepdims=False)
        for shift in range(1, n_wide):
            perm = [(i, (i + shift) % n_wide) for i in range(n_wide)]
            piece = lax.dynamic_index_in_dim(part, (w + shift) % n_wide, 0, keepdims=False)
            summed = summed + lax.ppermute(piece, "wide", perm)
        part = summed
        part = part.reshape(pairs_w, rows, span, b_blk)
        flipped = jnp.concatenate(
            [part[:, :, (span - k) % span : (span - k) % span + 1] for k in range(span)] * 2, axis=2
        )
        ordered = lax.dynamic_slice_in_dim(flipped, span - r, span, 2)
        n_per_w = n_narrow // n_wide
        w_per_g = n_wide // GROUPS
        cols = span * b_blk // w_per_g
        ordered = ordered.reshape(n_per_w, pairs_w // n_per_w, rows, w_per_g, cols)
        ladder = None
        for t in range(span):
            k = (t + r) % span
            piece = lax.dynamic_index_in_dim(ordered, k // w_per_g, 0, keepdims=False)
            piece = lax.dynamic_index_in_dim(piece, k % w_per_g, 2, keepdims=False)
            perm = []
            for gg in range(GROUPS):
                for rr in range(span):
                    for ww in range(n_wide):
                        kk = (t + rr) % span
                        dst_n = ww * n_per_w + kk // w_per_g
                        dst_w = gg * w_per_g + kk % w_per_g
                        perm.append(((gg * span + rr) * n_wide + ww, dst_n * n_wide + dst_w))
            piece = lax.ppermute(piece, ("narrow", "wide"), perm)
            ladder = piece if ladder is None else ladder + piece

        local_cols = ladder.shape[2]
        occ_ids = jnp.arange(occ_energy.shape[0], dtype=jnp.int32)
        occ_first = jnp.sum(
            jnp.where(pair_list[:, 0:1] == occ_ids[None, :], occ_energy[None, :], 0.0), axis=1
        )
        occ_second = jnp.sum(
            jnp.where(pair_list[:, 1:2] == occ_ids[None, :], occ_energy[None, :], 0.0), axis=1
        )
        vir_cols = lax.dynamic_slice_in_dim(vir_energy, w * local_cols, local_cols, 0)
        vir_rows = vir_energy[:rows]
        denominator = (
            (occ_first + occ_second)[:, None, None] - vir_rows[None, :, None] - vir_cols[None, None, :]
        )
        return ladder / denominator

    return body


def solution(mesh):
    return jax.shard_map(
        make_body(mesh.shape["narrow"], mesh.shape["wide"]),
        mesh=mesh,
        in_specs=(
            P(None, "narrow", "wide"),
            P(None, "narrow", None),
            P("narrow", "wide", None),
            P("narrow", None),
            P(),
            P(),
        ),
        out_specs=P("narrow", None, "wide"),
        check_vma=False,
    )
```

```python
import jax
import jax.numpy as jnp
from jax import lax
from jax.sharding import PartitionSpec as P

GROUPS = 2


def make_body(n_narrow, n_wide):
    span = n_narrow // GROUPS

    def body(amps, left_fit, right_fit, pair_list, occ_energy, vir_energy):
        n = lax.axis_index("narrow")
        w = lax.axis_index("wide")
        r = n % span
        g = n // span
        b_blk, d_blk, aux = right_fit.shape
        q_blk = aux // span
        rows, c_blk, _ = left_fit.shape
        pairs = amps.shape[0]
        vir_total = b_blk * n_narrow

        def perm_of(shift, step):
            return [
                (gg * span + i, ((gg + step) % GROUPS) * span + (i + shift) % span)
                for gg in range(GROUPS)
                for i in range(span)
            ]

        own_set = [amps] + [lax.ppermute(amps, "narrow", perm_of(0, step)) for step in range(1, GROUPS)]
        group_set = jnp.stack(own_set, axis=0)
        right_split = right_fit.reshape(b_blk, d_blk, span, q_blk)
        set_size = group_set.size
        shifted_sets = [group_set]
        chunks = [lax.dynamic_index_in_dim(right_split, r, 2, keepdims=False)]
        for shift in range(1, span):
            piece = lax.dynamic_index_in_dim(right_split, (r + shift) % span, 2, keepdims=False)
            both = jnp.concatenate([group_set.reshape(-1), piece.reshape(-1)])
            both = lax.ppermute(both, "narrow", perm_of(shift, 0))
            shifted_sets.append(both[:set_size].reshape(group_set.shape))
            chunks.append(both[set_size:].reshape(piece.shape))
        amps_all = jnp.stack(shifted_sets, axis=1)

        def rotate_back(x, by, size, axis):
            rev = [lax.slice_in_dim(x, (size - j) % size, (size - j) % size + 1, axis=axis) for j in range(size)]
            return lax.dynamic_slice_in_dim(jnp.concatenate(rev * 2, axis=axis), size - by, size, axis)

        c_sub = c_blk // n_wide
        left_part = lax.dynamic_slice_in_dim(left_fit, w * c_sub, c_sub, 1)
        left_part = left_part.reshape(rows, c_sub, span, q_blk).transpose(2, 3, 1, 0)
        left_send = jnp.concatenate([left_part] * GROUPS, axis=0)
        left_recv = lax.all_to_all(left_send, "narrow", 0, 0, tiled=True)
        left_recv = left_recv.reshape((GROUPS, span) + left_recv.shape[1:])
        left_recv = rotate_back(rotate_back(left_recv, r, span, 1), g, GROUPS, 0)
        left_recv = left_recv.reshape((n_narrow,) + left_recv.shape[2:])
        left_all = lax.all_gather(left_recv, "wide", axis=0, tiled=False)
        amps_all = amps_all.reshape(n_narrow, pairs, n_wide, c_sub, amps.shape[2])

        inter = jnp.einsum(
            "wkqia,kpwid->padq", left_all, amps_all, preferred_element_type=jnp.float32
        ).astype(jnp.bfloat16)

        right_group = jnp.concatenate(chunks, axis=0)
        part = jnp.einsum(
            "padq,bdq->pab", inter, right_group, preferred_element_type=jnp.float32
        )
        pairs_w = pairs // n_wide
        part = part.reshape(n_wide, pairs_w, rows, span * b_blk)
        summed = lax.dynamic_index_in_dim(part, w, 0, keepdims=False)
        for shift in range(1, n_wide):
            perm = [(i, (i + shift) % n_wide) for i in range(n_wide)]
            piece = lax.dynamic_index_in_dim(part, (w + shift) % n_wide, 0, keepdims=False)
            summed = summed + lax.ppermute(piece, "wide", perm)
        part = summed
        part = part.reshape(pairs_w, rows, span, b_blk)
        flipped = jnp.concatenate(
            [part[:, :, (span - k) % span : (span - k) % span + 1] for k in range(span)] * 2, axis=2
        )
        ordered = lax.dynamic_slice_in_dim(flipped, span - r, span, 2)
        n_per_w = n_narrow // n_wide
        w_per_g = n_wide // GROUPS
        cols = span * b_blk // w_per_g
        ordered = ordered.reshape(n_per_w, pairs_w // n_per_w, rows, w_per_g, cols)
        ladder = None
        for t in range(span):
            k = (t + r) % span
            piece = lax.dynamic_index_in_dim(ordered, k // w_per_g, 0, keepdims=False)
            piece = lax.dynamic_index_in_dim(piece, k % w_per_g, 2, keepdims=False)
            perm = []
            for gg in range(GROUPS):
                for rr in range(span):
                    for ww in range(n_wide):
                        kk = (t + rr) % span
                        dst_n = ww * n_per_w + kk // w_per_g
                        dst_w = gg * w_per_g + kk % w_per_g
                        perm.append(((gg * span + rr) * n_wide + ww, dst_n * n_wide + dst_w))
            piece = lax.ppermute(piece, ("narrow", "wide"), perm)
            ladder = piece if ladder is None else ladder + piece

        local_cols = ladder.shape[2]
        occ_ids = jnp.arange(occ_energy.shape[0], dtype=jnp.int32)
        occ_first = jnp.sum(
            jnp.where(pair_list[:, 0:1] == occ_ids[None, :], occ_energy[None, :], 0.0), axis=1
        )
        occ_second = jnp.sum(
            jnp.where(pair_list[:, 1:2] == occ_ids[None, :], occ_energy[None, :], 0.0), axis=1
        )
        vir_cols = lax.dynamic_slice_in_dim(vir_energy, w * local_cols, local_cols, 0)
        vir_rows = vir_energy[:rows]
        denominator = (
            (occ_first + occ_second)[:, None, None] - vir_rows[None, :, None] - vir_cols[None, None, :]
        )
        return ladder / denominator

    return body


def solution(mesh):
    return jax.shard_map(
        make_body(mesh.shape["narrow"], mesh.shape["wide"]),
        mesh=mesh,
        in_specs=(
            P(None, "narrow", "wide"),
            P(None, "narrow", None),
            P("narrow", "wide", None),
            P("narrow", None),
            P(),
            P(),
        ),
        out_specs=P("narrow", None, "wide"),
        check_vma=False,
    )
```

```python
import jax
import jax.numpy as jnp
from jax import lax
from jax.sharding import PartitionSpec as P

GROUPS = 2


def make_body(n_narrow, n_wide):
    span = n_narrow // GROUPS

    def body(amps, left_fit, right_fit, pair_list, occ_energy, vir_energy):
        n = lax.axis_index("narrow")
        w = lax.axis_index("wide")
        r = n % span
        g = n // span
        b_blk, d_blk, aux = right_fit.shape
        q_blk = aux // span
        rows, c_blk, _ = left_fit.shape
        pairs = amps.shape[0]
        vir_total = b_blk * n_narrow

        def perm_of(shift, step):
            return [
                (gg * span + i, ((gg + step) % GROUPS) * span + (i + shift) % span)
                for gg in range(GROUPS)
                for i in range(span)
            ]

        own_set = [amps] + [lax.ppermute(amps, "narrow", perm_of(0, step)) for step in range(1, GROUPS)]
        group_set = jnp.stack(own_set, axis=0)
        shifted_sets = [group_set] + [
            lax.ppermute(group_set, "narrow", perm_of(shift, 0)) for shift in range(1, span)
        ]
        amps_all = jnp.stack(shifted_sets, axis=1)

        def rotate_back(x, by, size, axis):
            rev = [lax.slice_in_dim(x, (size - j) % size, (size - j) % size + 1, axis=axis) for j in range(size)]
            return lax.dynamic_slice_in_dim(jnp.concatenate(rev * 2, axis=axis), size - by, size, axis)

        c_sub = c_blk // n_wide
        left_part = lax.dynamic_slice_in_dim(left_fit, w * c_sub, c_sub, 1)
        left_part = left_part.reshape(rows, c_sub, span, q_blk).transpose(2, 3, 1, 0)
        left_send = jnp.concatenate([left_part] * GROUPS, axis=0)
        left_recv = lax.all_to_all(left_send, "narrow", 0, 0, tiled=True)
        left_recv = left_recv.reshape((GROUPS, span) + left_recv.shape[1:])
        left_recv = rotate_back(rotate_back(left_recv, r, span, 1), g, GROUPS, 0)
        left_recv = left_recv.reshape((n_narrow,) + left_recv.shape[2:])
        left_all = lax.all_gather(left_recv, "wide", axis=0, tiled=False)
        amps_all = amps_all.reshape(n_narrow, pairs, n_wide, c_sub, amps.shape[2])

        right_split = right_fit.reshape(b_blk, d_blk, span, q_blk)
        chunks = []
        for shift in range(span):
            dest = (r + shift) % span
            piece = lax.dynamic_index_in_dim(right_split, dest, 2, keepdims=False)
            if shift:
                perm = [
                    (gg * span + i, gg * span + (i + shift) % span)
                    for gg in range(GROUPS)
                    for i in range(span)
                ]
                piece = lax.ppermute(piece, "narrow", perm)
            chunks.append(piece)

        inter = jnp.einsum(
            "wkqia,kpwid->padq", left_all, amps_all, preferred_element_type=jnp.float32
        ).astype(jnp.bfloat16)

        right_group = jnp.concatenate(chunks, axis=0)
        pairs_w = pairs // n_wide
        summed = None
        for shift in list(range(1, n_wide)) + [0]:
            blk = (w + shift) % n_wide
            inter_blk = lax.dynamic_slice_in_dim(inter, blk * pairs_w, pairs_w, 0)
            piece = jnp.einsum(
                "padq,bdq->pab", inter_blk, right_group, preferred_element_type=jnp.float32
            )
            if shift:
                perm = [(i, (i + shift) % n_wide) for i in range(n_wide)]
                piece = lax.ppermute(piece, "wide", perm)
            summed = piece if summed is None else summed + piece
        part = summed
        part = part.reshape(pairs_w, rows, span, b_blk)
        flipped = jnp.concatenate(
            [part[:, :, (span - k) % span : (span - k) % span + 1] for k in range(span)] * 2, axis=2
        )
        ordered = lax.dynamic_slice_in_dim(flipped, span - r, span, 2)
        n_per_w = n_narrow // n_wide
        w_per_g = n_wide // GROUPS
        cols = span * b_blk // w_per_g
        ordered = ordered.reshape(n_per_w, pairs_w // n_per_w, rows, w_per_g, cols)
        ladder = None
        for t in range(span):
            k = (t + r) % span
            piece = lax.dynamic_index_in_dim(ordered, k // w_per_g, 0, keepdims=False)
            piece = lax.dynamic_index_in_dim(piece, k % w_per_g, 2, keepdims=False)
            perm = []
            for gg in range(GROUPS):
                for rr in range(span):
                    for ww in range(n_wide):
                        kk = (t + rr) % span
                        dst_n = ww * n_per_w + kk // w_per_g
                        dst_w = gg * w_per_g + kk % w_per_g
                        perm.append(((gg * span + rr) * n_wide + ww, dst_n * n_wide + dst_w))
            piece = lax.ppermute(piece, ("narrow", "wide"), perm)
            ladder = piece if ladder is None else ladder + piece

        local_cols = ladder.shape[2]
        occ_ids = jnp.arange(occ_energy.shape[0], dtype=jnp.int32)
        occ_first = jnp.sum(
            jnp.where(pair_list[:, 0:1] == occ_ids[None, :], occ_energy[None, :], 0.0), axis=1
        )
        occ_second = jnp.sum(
            jnp.where(pair_list[:, 1:2] == occ_ids[None, :], occ_energy[None, :], 0.0), axis=1
        )
        vir_cols = lax.dynamic_slice_in_dim(vir_energy, w * local_cols, local_cols, 0)
        vir_rows = vir_energy[:rows]
        denominator = (
            (occ_first + occ_second)[:, None, None] - vir_rows[None, :, None] - vir_cols[None, None, :]
        )
        return ladder / denominator

    return body


def solution(mesh):
    return jax.shard_map(
        make_body(mesh.shape["narrow"], mesh.shape["wide"]),
        mesh=mesh,
        in_specs=(
            P(None, "narrow", "wide"),
            P(None, "narrow", None),
            P("narrow", "wide", None),
            P("narrow", None),
            P(),
            P(),
        ),
        out_specs=P("narrow", None, "wide"),
        check_vma=False,
    )
```

```python
import jax
import jax.numpy as jnp
from jax import lax
from jax.sharding import PartitionSpec as P

GROUPS = 2


def make_body(n_narrow, n_wide):
    span = n_narrow // GROUPS

    def body(amps, left_fit, right_fit, pair_list, occ_energy, vir_energy):
        n = lax.axis_index("narrow")
        w = lax.axis_index("wide")
        r = n % span
        g = n // span
        b_blk, d_blk, aux = right_fit.shape
        q_blk = aux // span
        rows, c_blk, _ = left_fit.shape
        pairs = amps.shape[0]
        vir_total = b_blk * n_narrow

        def perm_of(shift, step):
            return [
                (gg * span + i, ((gg + step) % GROUPS) * span + (i + shift) % span)
                for gg in range(GROUPS)
                for i in range(span)
            ]

        own_set = [amps] + [lax.ppermute(amps, "narrow", perm_of(0, step)) for step in range(1, GROUPS)]
        group_set = jnp.stack(own_set, axis=0)
        shifted_sets = [group_set] + [
            lax.ppermute(group_set, "narrow", perm_of(shift, 0)) for shift in range(1, span)
        ]
        amps_all = jnp.stack(shifted_sets, axis=1)

        def rotate_back(x, by, size, axis):
            rev = [lax.slice_in_dim(x, (size - j) % size, (size - j) % size + 1, axis=axis) for j in range(size)]
            return lax.dynamic_slice_in_dim(jnp.concatenate(rev * 2, axis=axis), size - by, size, axis)

        c_half = c_blk // 2
        core = w % 2
        left_part = lax.dynamic_slice_in_dim(left_fit, core * c_half, c_half, 1)
        left_part = left_part.reshape(rows, c_half, span, q_blk).transpose(2, 3, 1, 0)
        left_send = jnp.concatenate([left_part] * GROUPS, axis=0)
        left_recv = lax.all_to_all(left_send, "narrow", 0, 0, tiled=True)
        left_recv = left_recv.reshape((GROUPS, span) + left_recv.shape[1:])
        left_recv = rotate_back(rotate_back(left_recv, r, span, 1), g, GROUPS, 0)
        left_recv = left_recv.reshape((n_narrow,) + left_recv.shape[2:])
        partner = lax.ppermute(left_recv, "wide", [(i, i ^ 1) for i in range(n_wide)])
        left_all = jnp.stack(
            [jnp.where(core == 0, left_recv, partner), jnp.where(core == 0, partner, left_recv)], axis=0
        )
        amps_all = amps_all.reshape(n_narrow, pairs, 2, c_half, amps.shape[2])

        right_split = right_fit.reshape(b_blk, d_blk, span, q_blk)
        chunks = []
        for shift in range(span):
            dest = (r + shift) % span
            piece = lax.dynamic_index_in_dim(right_split, dest, 2, keepdims=False)
            if shift:
                perm = [
                    (gg * span + i, gg * span + (i + shift) % span)
                    for gg in range(GROUPS)
                    for i in range(span)
                ]
                piece = lax.ppermute(piece, "narrow", perm)
            chunks.append(piece)

        inter = jnp.einsum(
            "hkqia,kphid->padq", left_all, amps_all, preferred_element_type=jnp.float32
        ).astype(jnp.bfloat16)

        right_group = jnp.concatenate(chunks, axis=0)
        part = jnp.einsum(
            "padq,bdq->pab", inter, right_group, preferred_element_type=jnp.float32
        )
        pairs_w = pairs // n_wide
        part = part.reshape(n_wide, pairs_w, rows, span * b_blk)
        summed = lax.dynamic_index_in_dim(part, w, 0, keepdims=False)
        for shift in range(1, n_wide):
            perm = [(i, (i + shift) % n_wide) for i in range(n_wide)]
            piece = lax.dynamic_index_in_dim(part, (w + shift) % n_wide, 0, keepdims=False)
            summed = summed + lax.ppermute(piece, "wide", perm)
        part = summed
        part = part.reshape(pairs_w, rows, span, b_blk)
        flipped = jnp.concatenate(
            [part[:, :, (span - k) % span : (span - k) % span + 1] for k in range(span)] * 2, axis=2
        )
        ordered = lax.dynamic_slice_in_dim(flipped, span - r, span, 2)
        n_per_w = n_narrow // n_wide
        w_per_g = n_wide // GROUPS
        cols = span * b_blk // w_per_g
        ordered = ordered.reshape(n_per_w, pairs_w // n_per_w, rows, w_per_g, cols)
        ladder = None
        for t in range(span):
            k = (t + r) % span
            piece = lax.dynamic_index_in_dim(ordered, k // w_per_g, 0, keepdims=False)
            piece = lax.dynamic_index_in_dim(piece, k % w_per_g, 2, keepdims=False)
            perm = []
            for gg in range(GROUPS):
                for rr in range(span):
                    for ww in range(n_wide):
                        kk = (t + rr) % span
                        dst_n = ww * n_per_w + kk // w_per_g
                        dst_w = gg * w_per_g + kk % w_per_g
                        perm.append(((gg * span + rr) * n_wide + ww, dst_n * n_wide + dst_w))
            piece = lax.ppermute(piece, ("narrow", "wide"), perm)
            ladder = piece if ladder is None else ladder + piece

        local_cols = ladder.shape[2]
        occ_ids = jnp.arange(occ_energy.shape[0], dtype=jnp.int32)
        occ_first = jnp.sum(
            jnp.where(pair_list[:, 0:1] == occ_ids[None, :], occ_energy[None, :], 0.0), axis=1
        )
        occ_second = jnp.sum(
            jnp.where(pair_list[:, 1:2] == occ_ids[None, :], occ_energy[None, :], 0.0), axis=1
        )
        vir_cols = lax.dynamic_slice_in_dim(vir_energy, w * local_cols, local_cols, 0)
        vir_rows = vir_energy[:rows]
        denominator = (
            (occ_first + occ_second)[:, None, None] - vir_rows[None, :, None] - vir_cols[None, None, :]
        )
        return ladder / denominator

    return body


def solution(mesh):
    return jax.shard_map(
        make_body(mesh.shape["narrow"], mesh.shape["wide"]),
        mesh=mesh,
        in_specs=(
            P(None, "narrow", "wide"),
            P(None, "narrow", None),
            P("narrow", "wide", None),
            P("narrow", None),
            P(),
            P(),
        ),
        out_specs=P("narrow", None, "wide"),
        check_vma=False,
    )
```

```python
import jax
import jax.numpy as jnp
from jax import lax
from jax.sharding import PartitionSpec as P

GROUPS = 2


def make_body(n_narrow, n_wide):
    span = n_narrow // GROUPS

    def body(amps, left_fit, right_fit, pair_list, occ_energy, vir_energy):
        n = lax.axis_index("narrow")
        w = lax.axis_index("wide")
        r = n % span
        g = n // span
        b_blk, d_blk, aux = right_fit.shape
        q_blk = aux // span
        rows, c_blk, _ = left_fit.shape
        pairs = amps.shape[0]
        vir_total = b_blk * n_narrow

        def perm_of(shift, step):
            return [
                (gg * span + i, ((gg + step) % GROUPS) * span + (i + shift) % span)
                for gg in range(GROUPS)
                for i in range(span)
            ]

        own_set = [amps] + [lax.ppermute(amps, "narrow", perm_of(0, step)) for step in range(1, GROUPS)]
        group_set = jnp.stack(own_set, axis=0)
        shifted_sets = [group_set] + [
            lax.ppermute(group_set, "narrow", perm_of(shift, 0)) for shift in range(1, span)
        ]
        amps_all = jnp.stack(shifted_sets, axis=1)

        def rotate_back(x, by, size, axis):
            rev = [lax.slice_in_dim(x, (size - j) % size, (size - j) % size + 1, axis=axis) for j in range(size)]
            return lax.dynamic_slice_in_dim(jnp.concatenate(rev * 2, axis=axis), size - by, size, axis)

        c_sub = c_blk // n_wide
        left_part = lax.dynamic_slice_in_dim(left_fit, w * c_sub, c_sub, 1)
        left_part = left_part.reshape(rows, c_sub, span, q_blk).transpose(2, 3, 1, 0)
        left_send = jnp.concatenate([left_part] * GROUPS, axis=0)
        left_recv = lax.all_to_all(left_send, "narrow", 0, 0, tiled=True)
        left_recv = left_recv.reshape((GROUPS, span) + left_recv.shape[1:])
        left_recv = rotate_back(rotate_back(left_recv, r, span, 1), g, GROUPS, 0)
        left_recv = left_recv.reshape((n_narrow,) + left_recv.shape[2:])
        left_all = lax.all_gather(left_recv, "wide", axis=2, tiled=True)
        amps_all = amps_all.reshape(n_narrow, pairs, c_blk, amps.shape[2])

        right_split = right_fit.reshape(b_blk, d_blk, span, q_blk)
        chunks = []
        for shift in range(span):
            dest = (r + shift) % span
            piece = lax.dynamic_index_in_dim(right_split, dest, 2, keepdims=False)
            if shift:
                perm = [
                    (gg * span + i, gg * span + (i + shift) % span)
                    for gg in range(GROUPS)
                    for i in range(span)
                ]
                piece = lax.ppermute(piece, "narrow", perm)
            chunks.append(piece)

        inter = jnp.einsum(
            "kqca,kpcd->padq", left_all, amps_all, preferred_element_type=jnp.float32
        ).astype(jnp.bfloat16)

        right_group = jnp.concatenate(chunks, axis=0)
        part = jnp.einsum(
            "padq,bdq->pab", inter, right_group, preferred_element_type=jnp.float32
        )
        pairs_w = pairs // n_wide
        part = part.reshape(n_wide, pairs_w, rows, span * b_blk)
        summed = lax.dynamic_index_in_dim(part, w, 0, keepdims=False)
        for shift in range(1, n_wide):
            perm = [(i, (i + shift) % n_wide) for i in range(n_wide)]
            piece = lax.dynamic_index_in_dim(part, (w + shift) % n_wide, 0, keepdims=False)
            summed = summed + lax.ppermute(piece, "wide", perm)
        part = summed
        part = part.reshape(pairs_w, rows, span, b_blk)
        flipped = jnp.concatenate(
            [part[:, :, (span - k) % span : (span - k) % span + 1] for k in range(span)] * 2, axis=2
        )
        ordered = lax.dynamic_slice_in_dim(flipped, span - r, span, 2)
        n_per_w = n_narrow // n_wide
        w_per_g = n_wide // GROUPS
        cols = span * b_blk // w_per_g
        ordered = ordered.reshape(n_per_w, pairs_w // n_per_w, rows, w_per_g, cols)
        ladder = None
        for t in range(span):
            k = (t + r) % span
            piece = lax.dynamic_index_in_dim(ordered, k // w_per_g, 0, keepdims=False)
            piece = lax.dynamic_index_in_dim(piece, k % w_per_g, 2, keepdims=False)
            perm = []
            for gg in range(GROUPS):
                for rr in range(span):
                    for ww in range(n_wide):
                        kk = (t + rr) % span
                        dst_n = ww * n_per_w + kk // w_per_g
                        dst_w = gg * w_per_g + kk % w_per_g
                        perm.append(((gg * span + rr) * n_wide + ww, dst_n * n_wide + dst_w))
            piece = lax.ppermute(piece, ("narrow", "wide"), perm)
            ladder = piece if ladder is None else ladder + piece

        local_cols = ladder.shape[2]
        occ_ids = jnp.arange(occ_energy.shape[0], dtype=jnp.int32)
        occ_first = jnp.sum(
            jnp.where(pair_list[:, 0:1] == occ_ids[None, :], occ_energy[None, :], 0.0), axis=1
        )
        occ_second = jnp.sum(
            jnp.where(pair_list[:, 1:2] == occ_ids[None, :], occ_energy[None, :], 0.0), axis=1
        )
        vir_cols = lax.dynamic_slice_in_dim(vir_energy, w * local_cols, local_cols, 0)
        vir_rows = vir_energy[:rows]
        denominator = (
            (occ_first + occ_second)[:, None, None] - vir_rows[None, :, None] - vir_cols[None, None, :]
        )
        return ladder / denominator

    return body


def solution(mesh):
    return jax.shard_map(
        make_body(mesh.shape["narrow"], mesh.shape["wide"]),
        mesh=mesh,
        in_specs=(
            P(None, "narrow", "wide"),
            P(None, "narrow", None),
            P("narrow", "wide", None),
            P("narrow", None),
            P(),
            P(),
        ),
        out_specs=P("narrow", None, "wide"),
        check_vma=False,
    )
```

```python
import jax
import jax.numpy as jnp
from jax import lax
from jax.sharding import PartitionSpec as P

GROUPS = 2


def make_body(n_narrow, n_wide):
    span = n_narrow // GROUPS

    def body(amps, left_fit, right_fit, pair_list, occ_energy, vir_energy):
        n = lax.axis_index("narrow")
        w = lax.axis_index("wide")
        r = n % span
        g = n // span
        b_blk, d_blk, aux = right_fit.shape
        q_blk = aux // span
        rows, c_blk, _ = left_fit.shape
        pairs = amps.shape[0]
        vir_total = b_blk * n_narrow

        def perm_of(shift, step):
            return [
                (gg * span + i, ((gg + step) % GROUPS) * span + (i + shift) % span)
                for gg in range(GROUPS)
                for i in range(span)
            ]

        own_set = [amps] + [lax.ppermute(amps, "narrow", perm_of(0, step)) for step in range(1, GROUPS)]
        group_set = jnp.stack(own_set, axis=0)
        shifted_sets = [group_set] + [
            lax.ppermute(group_set, "narrow", perm_of(shift, 0)) for shift in range(1, span)
        ]
        amps_all = jnp.stack(shifted_sets, axis=1)

        def rotate_back(x, by, size, axis):
            rev = [lax.slice_in_dim(x, (size - j) % size, (size - j) % size + 1, axis=axis) for j in range(size)]
            return lax.dynamic_slice_in_dim(jnp.concatenate(rev * 2, axis=axis), size - by, size, axis)

        c_sub = c_blk // n_wide
        left_part = lax.dynamic_slice_in_dim(left_fit, w * c_sub, c_sub, 1)
        left_part = left_part.reshape(rows, c_sub, span, q_blk).transpose(2, 3, 1, 0)
        left_send = jnp.concatenate([left_part] * GROUPS, axis=0)
        left_recv = lax.all_to_all(left_send, "narrow", 0, 0, tiled=True)
        left_recv = left_recv.reshape((GROUPS, span) + left_recv.shape[1:])
        left_recv = rotate_back(rotate_back(left_recv, r, span, 1), g, GROUPS, 0)
        left_recv = left_recv.reshape((n_narrow,) + left_recv.shape[2:])
        left_all = lax.all_gather(left_recv, "wide", axis=0, tiled=False)
        amps_all = amps_all.reshape(n_narrow, pairs, n_wide, c_sub, amps.shape[2])

        right_split = right_fit.reshape(b_blk, d_blk, span, q_blk)
        chunks = []
        for shift in range(span):
            dest = (r + shift) % span
            piece = lax.dynamic_index_in_dim(right_split, dest, 2, keepdims=False)
            if shift:
                perm = [
                    (gg * span + i, gg * span + (i + shift) % span)
                    for gg in range(GROUPS)
                    for i in range(span)
                ]
                piece = lax.ppermute(piece, "narrow", perm)
            chunks.append(piece)

        inter = jnp.einsum(
            "wkqia,kpwid->padq", left_all, amps_all, preferred_element_type=jnp.float32
        ).astype(jnp.bfloat16)

        right_group = jnp.concatenate(chunks, axis=0)
        part = jnp.einsum(
            "padq,bdq->pab", inter, right_group, preferred_element_type=jnp.float32
        )
        pairs_w = pairs // n_wide
        part = part.reshape(n_wide, pairs_w, rows, span * b_blk)
        summed = lax.dynamic_index_in_dim(part, w, 0, keepdims=False)
        for shift in range(1, n_wide):
            perm = [(i, (i + shift) % n_wide) for i in range(n_wide)]
            piece = lax.dynamic_index_in_dim(part, (w + shift) % n_wide, 0, keepdims=False)
            summed = summed + lax.ppermute(piece, "wide", perm)
        part = summed
        n_per_w = n_narrow // n_wide
        w_per_g = n_wide // GROUPS
        blocks_per_col = span // w_per_g
        part = part.reshape(n_per_w, pairs_w // n_per_w, rows, span, b_blk)
        ladder = None
        for t in range(span):
            k = (t + r) % span
            sub = lax.dynamic_index_in_dim(part, k // w_per_g, 0, keepdims=False)
            col = k % w_per_g
            piece = jnp.concatenate(
                [
                    lax.dynamic_index_in_dim(sub, (r - col * blocks_per_col - m) % span, 2, keepdims=False)
                    for m in range(blocks_per_col)
                ],
                axis=2,
            )
            perm = []
            for gg in range(GROUPS):
                for rr in range(span):
                    for ww in range(n_wide):
                        kk = (t + rr) % span
                        dst_n = ww * n_per_w + kk // w_per_g
                        dst_w = gg * w_per_g + kk % w_per_g
                        perm.append(((gg * span + rr) * n_wide + ww, dst_n * n_wide + dst_w))
            piece = lax.ppermute(piece, ("narrow", "wide"), perm)
            ladder = piece if ladder is None else ladder + piece

        local_cols = ladder.shape[2]
        occ_ids = jnp.arange(occ_energy.shape[0], dtype=jnp.int32)
        occ_first = jnp.sum(
            jnp.where(pair_list[:, 0:1] == occ_ids[None, :], occ_energy[None, :], 0.0), axis=1
        )
        occ_second = jnp.sum(
            jnp.where(pair_list[:, 1:2] == occ_ids[None, :], occ_energy[None, :], 0.0), axis=1
        )
        vir_cols = lax.dynamic_slice_in_dim(vir_energy, w * local_cols, local_cols, 0)
        vir_rows = vir_energy[:rows]
        denominator = (
            (occ_first + occ_second)[:, None, None] - vir_rows[None, :, None] - vir_cols[None, None, :]
        )
        return ladder / denominator

    return body


def solution(mesh):
    return jax.shard_map(
        make_body(mesh.shape["narrow"], mesh.shape["wide"]),
        mesh=mesh,
        in_specs=(
            P(None, "narrow", "wide"),
            P(None, "narrow", None),
            P("narrow", "wide", None),
            P("narrow", None),
            P(),
            P(),
        ),
        out_specs=P("narrow", None, "wide"),
        check_vma=False,
    )
```
